32 devices in a mesh: dp: 8 (over y, x, core), mp: 4 (over z).
Axes of the slice: x: 2, y: 2, z: 4, core: 2. Of those that a mesh axis runs over, the one named last changes fastest.
Arguments:
- activations: bfloat16 [4, 16, 1024, 4096], P(None, 'dp', 'mp'), may hold values from -6 to 6
- cotangents: bfloat16 [4, 16, 1024, 4096], P(None, 'dp', 'mp'), may hold values from -0.1875 to 0.1875
- lengths: int32 [16], P('dp'), may hold values from 128 to 1024, as said below
- project_in: bfloat16 [4, 64, 4096], replicated, may hold values from -0.09375 to 0.09375
- project_out: bfloat16 [4, 64, 4096], replicated, may hold values from -0.09375 to 0.09375
- preconditioner: bfloat16 [16384, 4096], P('mp', 'dp'), as said below
- queries: bfloat16 [8192, 16384], P('dp', 'mp'), may hold values from -0.0625 to 0.0625
Outputs:
- scores: float32 [16, 8192], P(None, ('dp', 'mp'))
The draws below stay inside these ranges and needn't reach their ends.
Inputs may be any that keep to these rules, and one draw needn't show every extreme that they name: `lengths`: positions at or past an example's length are padding; some example has all 1024 positions live. `preconditioner`: each layer's 4096 x 4096 block is symmetric.
All inputs are finite; a program needn't handle non-finite values.
Results may differ from the reference program's by a relative error of at most 0.005.
Values may be sent and summed in bfloat16 or wider, within the bound.
No kernel may reach another device: no remote copies, remote signals or barrier semaphores. Data moves between devices by JAX's collectives and lax.ppermute only.
A program may use at most 128 MiB of HBM per device.

```python
import math
import jax
import jax.numpy as jnp
from jax import lax

D = 4096
KF = 64
LAYERS = 4
SEQ = 1024
K = 4096
FLAT = 16384
EXAMPLES = 16
QUERIES = 8192


def draw_lengths(key, part):
    first_key = jax.random.fold_in(key, 11)
    second_key = jax.random.fold_in(key, 12)
    base_lengths = jax.random.randint(first_key, (EXAMPLES,), SEQ // 8, SEQ + 1)
    chosen = jax.random.randint(second_key, (), 0, EXAMPLES)
    return jnp.where(jnp.arange(EXAMPLES) == chosen, SEQ, base_lengths).astype(jnp.int32)


def draw_preconditioner(key, part):
    first_key = jax.random.fold_in(key, 21)
    second_key = jax.random.fold_in(key, 22)
    raw_values = jax.random.normal(first_key, (LAYERS, K, K), jnp.float32)
    diag_values = jnp.exp(jax.random.uniform(second_key, (LAYERS, K), jnp.float32, math.log(0.5), math.log(2.0)))
    symmetric = (raw_values + jnp.swapaxes(raw_values, 1, 2)) * (0.7 / math.sqrt(2.0 * K))
    diagonal_mask = jnp.arange(K)[:, None] == jnp.arange(K)[None, :]
    blocks = jnp.where(diagonal_mask[None, :, :], diag_values[:, :, None], symmetric)
    return blocks.reshape(LAYERS * K, K).astype(jnp.bfloat16)


def strengthened(entries, rng, source, target, blocks, factor):
    def block_of(axis_at):
        return (jnp.arange(entries.shape[axis_at]) // (entries.shape[axis_at] // blocks)).reshape((-1,) + (1,) * (entries.ndim - 1 - axis_at))

    near = jax.random.permutation(rng, blocks)[block_of(target)]
    second = (block_of(target) + blocks // 2) % blocks
    return jnp.where((block_of(source) == near) | (block_of(source) == second), factor * entries, entries)


def levels(rng, extent, split, low, largest):
    factor_of = 1.0
    for position, shards_of in split:
        steps = jax.random.uniform(jax.random.fold_in(jax.random.fold_in(rng, 6), position), (shards_of,), jnp.float32, low / len(split), largest / len(split))
        factor_of = factor_of * jnp.repeat(jnp.exp(steps), extent[position] // shards_of).reshape((-1,) + (1,) * (len(extent) - 1 - position))
    return factor_of


def bell_draw(stream_key, shape, spread, bound, cuts=(), kind=jnp.bfloat16):
    loudness = levels(stream_key, shape, cuts, -0.22, 0.18) if cuts else 1.0
    entries = jax.random.normal(stream_key, shape, jnp.float32) * spread * loudness
    return jnp.minimum(jnp.maximum(entries, -bound), bound).astype(kind)


def heavy_noise(rng, shape, scale, most, shards, heavy, kind=jnp.bfloat16):
    result = scale * jax.random.normal(rng, shape, jnp.float32)
    if shards:
        result = result * levels(rng, shape, shards, -0.22, 0.18)
    return jnp.clip(strengthened(result, jax.random.fold_in(rng, 3), *heavy), -most, most).astype(kind)


def setup_inputs(seed: int = 0) -> dict:
    streams_of = jax.random.split(jax.random.key(seed), 8)
    return {
        "activations": bell_draw(streams_of[0], (LAYERS, EXAMPLES, SEQ, D), 1.0, 6.0, ((1, 8), (2, 4))),
        "cotangents": bell_draw(streams_of[1], (LAYERS, EXAMPLES, SEQ, D), SEQ ** -0.5, 0.1875, ((1, 8), (2, 4))),
        "lengths": draw_lengths(jax.random.fold_in(streams_of[7], 71), 0),
        "project_in": bell_draw(streams_of[3], (LAYERS, KF, D), D ** -0.5, 0.09375),
        "project_out": bell_draw(streams_of[4], (LAYERS, KF, D), D ** -0.5, 0.09375),
        "preconditioner": draw_preconditioner(jax.random.fold_in(streams_of[7], 71), 0),
        "queries": heavy_noise(streams_of[6], (QUERIES, FLAT), FLAT ** -0.5, 0.0625, ((0, 8), (1, 4)), (1, 0, 8, 2.0)),
    }


def split_parts(dense):
    upper = dense.astype(jnp.bfloat16)
    kept = lax.optimization_barrier(upper)
    lower = (dense - kept.astype(jnp.float32)).astype(jnp.bfloat16)
    return upper, lower


def reference(activations, cotangents, lengths, project_in, project_out, preconditioner, queries):
    positions = jnp.arange(SEQ, dtype=jnp.int32)
    live_mask = positions[None, :] < lengths[:, None]
    grad_blocks = []
    for layer_index in range(LAYERS):
        flat_acts = activations[layer_index].reshape(EXAMPLES * SEQ, D)
        flat_cot = cotangents[layer_index].reshape(EXAMPLES * SEQ, D)
        left_factor = jnp.dot(flat_acts, project_in[layer_index].T, preferred_element_type=jnp.float32).astype(jnp.bfloat16)
        right_factor = jnp.dot(flat_cot, project_out[layer_index].T, preferred_element_type=jnp.float32)
        right_factor = jnp.where(live_mask.reshape(EXAMPLES * SEQ, 1), right_factor, 0.0).astype(jnp.bfloat16)
        outer_sum = jnp.einsum("esj,esc->ejc", right_factor.astype(jnp.float32).reshape(EXAMPLES, SEQ, KF), left_factor.astype(jnp.float32).reshape(EXAMPLES, SEQ, KF))
        grad_blocks.append(outer_sum.reshape(EXAMPLES, K))
    grad_flat = jnp.concatenate(grad_blocks, axis=1).astype(jnp.bfloat16)
    scores = jnp.zeros((EXAMPLES, QUERIES), jnp.float32)
    for layer_index in range(LAYERS):
        layer_block = preconditioner[layer_index * K:(layer_index + 1) * K]
        grad_layer = grad_flat[:, layer_index * K:(layer_index + 1) * K]
        precond_grad = lax.dot_general(grad_layer, layer_block, (((1,), (1,)), ((), ())), preferred_element_type=jnp.float32)
        query_layer = queries[:, layer_index * K:(layer_index + 1) * K]
        upper, lower = split_parts(precond_grad)
        dims = (((1,), (1,)), ((), ()))
        scores = scores + lax.dot_general(upper, query_layer, dims, preferred_element_type=jnp.float32) + lax.dot_general(lower, query_layer, dims, preferred_element_type=jnp.float32)
    return scores
```

```python
import jax
import jax.numpy as jnp
from jax import lax
from jax.sharding import PartitionSpec as P


def split_parts(dense):
    upper = dense.astype(jnp.bfloat16)
    kept = lax.optimization_barrier(upper)
    lower = (dense - kept.astype(jnp.float32)).astype(jnp.bfloat16)
    return (upper, lower)


def shifted(x, axis, shift):
    n = lax.axis_size(axis)
    return lax.ppermute(x, axis, [(i, (i + shift) % n) for i in range(n)])


def reduce_scatter_direct(x, axis, dim):
    n = lax.axis_size(axis)
    me = lax.axis_index(axis)
    width = x.shape[dim] // n
    total = lax.dynamic_slice_in_dim(x, me * width, width, dim)
    for shift in range(1, n):
        piece = lax.dynamic_slice_in_dim(x, ((me + shift) % n) * width, width, dim)
        total = total + shifted(piece, axis, shift)
    return total


def all_gather_direct(x, axis):
    n = lax.axis_size(axis)
    me = lax.axis_index(axis)
    got = [x] + [shifted(x, axis, shift) for shift in range(1, n)]
    order = jnp.stack([got[(-k) % n] for k in range(n)])
    doubled = jnp.concatenate([order, order], axis=0)
    return lax.dynamic_slice_in_dim(doubled, (n - me) % n, n, 0)


def body_start(activations, cotangents, lengths, project_in, project_out, preconditioner, queries):
    width_mp = lax.axis_size("mp")
    layer_count = activations.shape[0]
    tokens_here = activations.shape[2]
    factor_size = project_in.shape[1]
    block_size = factor_size * factor_size
    group_size = width_mp // layer_count
    mp_place = lax.axis_index("mp")
    contract = (((1,), (1,)), ((), ()))
    positions = mp_place * tokens_here + jnp.arange(tokens_here, dtype=jnp.int32)
    live_mask = positions[None, :] < lengths[:, None]
    left_factor = jnp.einsum(
        "lesd,lkd->lesk", activations, project_in, preferred_element_type=jnp.float32
    ).astype(jnp.bfloat16)
    right_factor = jnp.einsum(
        "lesd,lkd->lesk", cotangents, project_out, preferred_element_type=jnp.float32
    )
    right_factor = jnp.where(live_mask[None, :, :, None], right_factor, 0.0).astype(jnp.bfloat16)
    partial_grad = jnp.einsum(
        "lesj,lesc->eljc", right_factor, left_factor, preferred_element_type=jnp.float32
    )
    partial_grad = partial_grad.reshape(partial_grad.shape[0], layer_count * block_size)
    grad_total = lax.psum(partial_grad, "mp")
    layer_place = mp_place // group_size
    grad_layer = lax.dynamic_slice_in_dim(
        grad_total, layer_place * block_size, block_size, 1
    ).astype(jnp.bfloat16)
    spread = lax.all_to_all(grad_layer, "dp", split_axis=1, concat_axis=0, tiled=True)
    partial_pre = lax.dot_general(
        spread, preconditioner, contract, preferred_element_type=jnp.float32
    )
    precond_grad = lax.psum(partial_pre, "dp")
    upper_grad, lower_grad = split_parts(precond_grad)
    scores = lax.psum_scatter(
        lax.dot_general(queries, upper_grad, contract, preferred_element_type=jnp.float32)
        + lax.dot_general(queries, lower_grad, contract, preferred_element_type=jnp.float32),
        "mp",
        scatter_dimension=0,
        tiled=True,
    )
    return scores.T


def body_direct(activations, cotangents, lengths, project_in, project_out, preconditioner, queries):
    layer_count = activations.shape[0]
    tokens_here = activations.shape[2]
    factor_size = project_in.shape[1]
    block_size = factor_size * factor_size
    width_dp = lax.axis_size("dp")
    mp_place = lax.axis_index("mp")
    positions = mp_place * tokens_here + jnp.arange(tokens_here, dtype=jnp.int32)
    live_mask = positions[None, :] < lengths[:, None]
    left_factor = jnp.einsum(
        "lesd,lkd->lesk", activations, project_in, preferred_element_type=jnp.float32
    ).astype(jnp.bfloat16)
    right_factor = jnp.einsum(
        "lesd,lkd->lesk", cotangents, project_out, preferred_element_type=jnp.float32
    )
    right_factor = jnp.where(live_mask[None, :, :, None], right_factor, 0.0).astype(jnp.bfloat16)
    partial_grad = jnp.einsum(
        "lesj,lesc->eljc", right_factor, left_factor, preferred_element_type=jnp.float32
    )
    partial_grad = partial_grad.reshape(partial_grad.shape[0], layer_count * block_size)
    grad_mine = reduce_scatter_direct(partial_grad, "mp", 1).astype(jnp.bfloat16)
    grad_all = all_gather_direct(grad_mine, "dp")
    grad_all = grad_all.reshape(-1, grad_all.shape[-1])
    pre_part = jnp.dot(grad_all, preconditioner, preferred_element_type=jnp.float32)
    pre_all = all_gather_direct(pre_part, "dp")
    pre_all = jnp.transpose(pre_all, (1, 0, 2)).reshape(pre_all.shape[1], -1)
    upper_grad, lower_grad = split_parts(pre_all)
    both = jnp.concatenate([upper_grad, lower_grad], axis=0)
    products = lax.dot_general(
        both, queries, (((1,), (1,)), ((), ())), preferred_element_type=jnp.float32
    )
    examples = upper_grad.shape[0]
    partial_scores = products[:examples] + products[examples:]
    return reduce_scatter_direct(partial_scores, "mp", 1)


def body(*args):
    layer_count = args[0].shape[0]
    if lax.axis_size("mp") == layer_count:
        return body_direct(*args)
    return body_start(*args)


def solution(mesh):
    return jax.shard_map(
        body,
        mesh=mesh,
        in_specs=(
            P(None, "dp", "mp", None),
            P(None, "dp", "mp", None),
            P("dp"),
            P(),
            P(),
            P("mp", "dp"),
            P("dp", "mp"),
        ),
        out_specs=P(None, ("dp", "mp")),
        check_vma=False,
    )
```

```python
import jax
import jax.numpy as jnp
from jax import lax
from jax.sharding import PartitionSpec as P


def split_parts(dense):
    upper = dense.astype(jnp.bfloat16)
    kept = lax.optimization_barrier(upper)
    lower = (dense - kept.astype(jnp.float32)).astype(jnp.bfloat16)
    return (upper, lower)


def shifted(x, axis, shift):
    n = lax.axis_size(axis)
    return lax.ppermute(x, axis, [(i, (i + shift) % n) for i in range(n)])


def reduce_scatter_direct(x, axis, dim):
    n = lax.axis_size(axis)
    me = lax.axis_index(axis)
    width = x.shape[dim] // n
    total = lax.dynamic_slice_in_dim(x, me * width, width, dim)
    for shift in range(1, n):
        piece = lax.dynamic_slice_in_dim(x, ((me + shift) % n) * width, width, dim)
        total = total + shifted(piece, axis, shift)
    return total


def all_gather_direct(x, axis):
    n = lax.axis_size(axis)
    me = lax.axis_index(axis)
    got = [x] + [shifted(x, axis, shift) for shift in range(1, n)]
    order = jnp.stack([got[(-k) % n] for k in range(n)])
    doubled = jnp.concatenate([order, order], axis=0)
    return lax.dynamic_slice_in_dim(doubled, (n - me) % n, n, 0)


def body_start(activations, cotangents, lengths, project_in, project_out, preconditioner, queries):
    width_mp = lax.axis_size("mp")
    layer_count = activations.shape[0]
    tokens_here = activations.shape[2]
    factor_size = project_in.shape[1]
    block_size = factor_size * factor_size
    group_size = width_mp // layer_count
    mp_place = lax.axis_index("mp")
    contract = (((1,), (1,)), ((), ()))
    positions = mp_place * tokens_here + jnp.arange(tokens_here, dtype=jnp.int32)
    live_mask = positions[None, :] < lengths[:, None]
    left_factor = jnp.einsum(
        "lesd,lkd->lesk", activations, project_in, preferred_element_type=jnp.float32
    ).astype(jnp.bfloat16)
    right_factor = jnp.einsum(
        "lesd,lkd->lesk", cotangents, project_out, preferred_element_type=jnp.float32
    )
    right_factor = jnp.where(live_mask[None, :, :, None], right_factor, 0.0).astype(jnp.bfloat16)
    partial_grad = jnp.einsum(
        "lesj,lesc->eljc", right_factor, left_factor, preferred_element_type=jnp.float32
    )
    partial_grad = partial_grad.reshape(partial_grad.shape[0], layer_count * block_size)
    grad_total = lax.psum(partial_grad, "mp")
    layer_place = mp_place // group_size
    grad_layer = lax.dynamic_slice_in_dim(
        grad_total, layer_place * block_size, block_size, 1
    ).astype(jnp.bfloat16)
    spread = lax.all_to_all(grad_layer, "dp", split_axis=1, concat_axis=0, tiled=True)
    partial_pre = lax.dot_general(
        spread, preconditioner, contract, preferred_element_type=jnp.float32
    )
    precond_grad = lax.psum(partial_pre, "dp")
    upper_grad, lower_grad = split_parts(precond_grad)
    scores = lax.psum_scatter(
        lax.dot_general(queries, upper_grad, contract, preferred_element_type=jnp.float32)
        + lax.dot_general(queries, lower_grad, contract, preferred_element_type=jnp.float32),
        "mp",
        scatter_dimension=0,
        tiled=True,
    )
    return scores.T


def layer_gradient(activations, cotangents, live_mask, project_in, project_out, layer):
    acts = lax.dynamic_index_in_dim(activations, layer, 0, keepdims=False)
    cots = lax.dynamic_index_in_dim(cotangents, layer, 0, keepdims=False)
    w_in = lax.dynamic_index_in_dim(project_in, layer, 0, keepdims=False)
    w_out = lax.dynamic_index_in_dim(project_out, layer, 0, keepdims=False)
    left_factor = jnp.einsum(
        "esd,kd->esk", acts, w_in, preferred_element_type=jnp.float32
    ).astype(jnp.bfloat16)
    right_factor = jnp.einsum(
        "esd,kd->esk", cots, w_out, preferred_element_type=jnp.float32
    )
    right_factor = jnp.where(live_mask[:, :, None], right_factor, 0.0).astype(jnp.bfloat16)
    grad = jnp.einsum(
        "esj,esc->ejc", right_factor, left_factor, preferred_element_type=jnp.float32
    )
    return grad.reshape(grad.shape[0], -1)


def body_direct(activations, cotangents, lengths, project_in, project_out, preconditioner, queries):
    layer_count = activations.shape[0]
    tokens_here = activations.shape[2]
    width_dp = lax.axis_size("dp")
    dp_place = lax.axis_index("dp")
    mp_place = lax.axis_index("mp")
    positions = mp_place * tokens_here + jnp.arange(tokens_here, dtype=jnp.int32)
    live_mask = positions[None, :] < lengths[:, None]
    grad_args = (activations, cotangents, live_mask, project_in, project_out)
    received = []
    for shift in range(1, layer_count):
        grad = layer_gradient(*grad_args, (mp_place + shift) % layer_count)
        received.append(shifted(grad, "mp", shift))
    grad_mine = layer_gradient(*grad_args, mp_place)
    for grad in received:
        grad_mine = grad_mine + grad
    grad_all = all_gather_direct(grad_mine.astype(jnp.bfloat16), "dp")
    grad_all = grad_all.reshape(-1, grad_all.shape[-1])
    pre_part = jnp.dot(grad_all, preconditioner, preferred_element_type=jnp.float32)
    upper_grad, lower_grad = split_parts(pre_part)
    both = jnp.concatenate([upper_grad, lower_grad], axis=0)
    block = both.shape[1]
    products = None
    for shift in range(width_dp):
        got = both if shift == 0 else shifted(both, "dp", shift)
        source = (dp_place - shift) % width_dp
        columns = lax.dynamic_slice_in_dim(queries, source * block, block, 1)
        term = lax.dot_general(
            got, columns, (((1,), (1,)), ((), ())), preferred_element_type=jnp.float32
        )
        products = term if products is None else products + term
    examples = upper_grad.shape[0]
    partial_scores = products[:examples] + products[examples:]
    return reduce_scatter_direct(partial_scores, "mp", 1)


def body(*args):
    layer_count = args[0].shape[0]
    if lax.axis_size("mp") == layer_count:
        return body_direct(*args)
    return body_start(*args)


def solution(mesh):
    return jax.shard_map(
        body,
        mesh=mesh,
        in_specs=(
            P(None, "dp", "mp", None),
            P(None, "dp", "mp", None),
            P("dp"),
            P(),
            P(),
            P("mp", "dp"),
            P("dp", "mp"),
        ),
        out_specs=P(None, ("dp", "mp")),
        check_vma=False,
    )
```

```python
import jax
import jax.numpy as jnp
from jax import lax
from jax.sharding import PartitionSpec as P


def split_parts(dense):
    upper = dense.astype(jnp.bfloat16)
    kept = lax.optimization_barrier(upper)
    lower = (dense - kept.astype(jnp.float32)).astype(jnp.bfloat16)
    return (upper, lower)


def shifted(x, axis, shift):
    n = lax.axis_size(axis)
    return lax.ppermute(x, axis, [(i, (i + shift) % n) for i in range(n)])


def reduce_scatter_direct(x, axis, dim):
    n = lax.axis_size(axis)
    me = lax.axis_index(axis)
    width = x.shape[dim] // n
    total = lax.dynamic_slice_in_dim(x, me * width, width, dim)
    for shift in range(1, n):
        piece = lax.dynamic_slice_in_dim(x, ((me + shift) % n) * width, width, dim)
        total = total + shifted(piece, axis, shift)
    return total


def all_gather_direct(x, axis):
    n = lax.axis_size(axis)
    me = lax.axis_index(axis)
    got = [x] + [shifted(x, axis, shift) for shift in range(1, n)]
    order = jnp.stack([got[(-k) % n] for k in range(n)])
    doubled = jnp.concatenate([order, order], axis=0)
    return lax.dynamic_slice_in_dim(doubled, (n - me) % n, n, 0)


def all_gather_a2a(x, axis):
    n = lax.axis_size(axis)
    copies = jnp.broadcast_to(x[None], (n,) + x.shape)
    return lax.all_to_all(copies, axis, 0, 0, tiled=True)


def body_start(activations, cotangents, lengths, project_in, project_out, preconditioner, queries):
    width_mp = lax.axis_size("mp")
    layer_count = activations.shape[0]
    tokens_here = activations.shape[2]
    factor_size = project_in.shape[1]
    block_size = factor_size * factor_size
    group_size = width_mp // layer_count
    mp_place = lax.axis_index("mp")
    contract = (((1,), (1,)), ((), ()))
    positions = mp_place * tokens_here + jnp.arange(tokens_here, dtype=jnp.int32)
    live_mask = positions[None, :] < lengths[:, None]
    left_factor = jnp.einsum(
        "lesd,lkd->lesk", activations, project_in, preferred_element_type=jnp.float32
    ).astype(jnp.bfloat16)
    right_factor = jnp.einsum(
        "lesd,lkd->lesk", cotangents, project_out, preferred_element_type=jnp.float32
    )
    right_factor = jnp.where(live_mask[None, :, :, None], right_factor, 0.0).astype(jnp.bfloat16)
    partial_grad = jnp.einsum(
        "lesj,lesc->eljc", right_factor, left_factor, preferred_element_type=jnp.float32
    )
    partial_grad = partial_grad.reshape(partial_grad.shape[0], layer_count * block_size)
    grad_total = lax.psum(partial_grad, "mp")
    layer_place = mp_place // group_size
    grad_layer = lax.dynamic_slice_in_dim(
        grad_total, layer_place * block_size, block_size, 1
    ).astype(jnp.bfloat16)
    spread = lax.all_to_all(grad_layer, "dp", split_axis=1, concat_axis=0, tiled=True)
    partial_pre = lax.dot_general(
        spread, preconditioner, contract, preferred_element_type=jnp.float32
    )
    precond_grad = lax.psum(partial_pre, "dp")
    upper_grad, lower_grad = split_parts(precond_grad)
    scores = lax.psum_scatter(
        lax.dot_general(queries, upper_grad, contract, preferred_element_type=jnp.float32)
        + lax.dot_general(queries, lower_grad, contract, preferred_element_type=jnp.float32),
        "mp",
        scatter_dimension=0,
        tiled=True,
    )
    return scores.T


def body_direct(activations, cotangents, lengths, project_in, project_out, preconditioner, queries):
    layer_count = activations.shape[0]
    tokens_here = activations.shape[2]
    factor_size = project_in.shape[1]
    block_size = factor_size * factor_size
    width_dp = lax.axis_size("dp")
    mp_place = lax.axis_index("mp")
    positions = mp_place * tokens_here + jnp.arange(tokens_here, dtype=jnp.int32)
    live_mask = positions[None, :] < lengths[:, None]
    left_factor = jnp.einsum(
        "lesd,lkd->lesk", activations, project_in, preferred_element_type=jnp.float32
    ).astype(jnp.bfloat16)
    right_factor = jnp.einsum(
        "lesd,lkd->lesk", cotangents, project_out, preferred_element_type=jnp.float32
    )
    right_factor = jnp.where(live_mask[None, :, :, None], right_factor, 0.0).astype(jnp.bfloat16)
    partial_grad = jnp.einsum(
        "lesj,lesc->eljc", right_factor, left_factor, preferred_element_type=jnp.float32
    )
    partial_grad = partial_grad.reshape(partial_grad.shape[0], layer_count * block_size)
    grad_mine = reduce_scatter_direct(partial_grad, "mp", 1).astype(jnp.bfloat16)
    grad_all = all_gather_a2a(grad_mine, "dp")
    grad_all = grad_all.reshape(-1, grad_all.shape[-1])
    pre_part = jnp.dot(grad_all, preconditioner, preferred_element_type=jnp.float32)
    upper_grad, lower_grad = split_parts(pre_part)
    both = jnp.concatenate([upper_grad, lower_grad], axis=0)
    both_all = all_gather_a2a(both, "dp")
    blocks, block = both_all.shape[0], both_all.shape[2]
    query_blocks = queries.reshape(queries.shape[0], blocks, block)
    products = lax.dot_general(
        both_all, query_blocks, (((0, 2), (1, 2)), ((), ())), preferred_element_type=jnp.float32
    )
    examples = upper_grad.shape[0]
    partial_scores = products[:examples] + products[examples:]
    return reduce_scatter_direct(partial_scores, "mp", 1)


def body(*args):
    layer_count = args[0].shape[0]
    if lax.axis_size("mp") == layer_count:
        return body_direct(*args)
    return body_start(*args)


def solution(mesh):
    return jax.shard_map(
        body,
        mesh=mesh,
        in_specs=(
            P(None, "dp", "mp", None),
            P(None, "dp", "mp", None),
            P("dp"),
            P(),
            P(),
            P("mp", "dp"),
            P("dp", "mp"),
        ),
        out_specs=P(None, ("dp", "mp")),
        check_vma=False,
    )
```

```python
import jax
import jax.numpy as jnp
from jax import lax
from jax.experimental import pallas as pl
from jax.experimental.pallas import tpu as pltpu
from jax.sharding import PartitionSpec as P


def split_parts(dense):
    upper = dense.astype(jnp.bfloat16)
    kept = lax.optimization_barrier(upper)
    lower = (dense - kept.astype(jnp.float32)).astype(jnp.bfloat16)
    return (upper, lower)


def shifted(x, axis, shift):
    n = lax.axis_size(axis)
    return lax.ppermute(x, axis, [(i, (i + shift) % n) for i in range(n)])


def reduce_scatter_direct(x, axis, dim):
    n = lax.axis_size(axis)
    me = lax.axis_index(axis)
    width = x.shape[dim] // n
    total = lax.dynamic_slice_in_dim(x, me * width, width, dim)
    for shift in range(1, n):
        piece = lax.dynamic_slice_in_dim(x, ((me + shift) % n) * width, width, dim)
        total = total + shifted(piece, axis, shift)
    return total


def all_gather_direct(x, axis):
    n = lax.axis_size(axis)
    me = lax.axis_index(axis)
    got = [x] + [shifted(x, axis, shift) for shift in range(1, n)]
    order = jnp.stack([got[(-k) % n] for k in range(n)])
    doubled = jnp.concatenate([order, order], axis=0)
    return lax.dynamic_slice_in_dim(doubled, (n - me) % n, n, 0)


def all_gather_a2a(x, axis):
    n = lax.axis_size(axis)
    copies = jnp.broadcast_to(x[None], (n,) + x.shape)
    return lax.all_to_all(copies, axis, 0, 0, tiled=True)


def gradient_kernel(limits_ref, act_ref, cot_ref, win_ref, wout_ref, out_ref):
    example = pl.program_id(1)
    nt = (((1,), (1,)), ((), ()))
    left = lax.dot_general(
        act_ref[...], win_ref[...], nt, preferred_element_type=jnp.float32
    ).astype(jnp.bfloat16)
    right = lax.dot_general(cot_ref[...], wout_ref[...], nt, preferred_element_type=jnp.float32)
    rows = lax.broadcasted_iota(jnp.int32, right.shape, 0)
    right = jnp.where(rows < limits_ref[example], right, 0.0).astype(jnp.bfloat16)
    out_ref[...] = lax.dot_general(
        right, left, (((0,), (0,)), ((), ())), preferred_element_type=jnp.float32
    )


def layer_gradients(activations, cotangents, limits, project_in, project_out):
    layers, examples, tokens, width = activations.shape
    factor = project_in.shape[1]
    data = pl.BlockSpec((None, None, tokens, width), lambda l, e, lim: (l, e, 0, 0))
    weights = pl.BlockSpec((None, factor, width), lambda l, e, lim: (l, 0, 0))
    flops = 4 * layers * examples * tokens * width * factor
    moved = 2 * (activations.size + cotangents.size + project_in.size + project_out.size)
    return pl.pallas_call(
        gradient_kernel,
        out_shape=jax.ShapeDtypeStruct((examples, layers, factor, factor), jnp.float32),
        grid_spec=pltpu.PrefetchScalarGridSpec(
            num_scalar_prefetch=1,
            grid=(layers, examples),
            in_specs=[data, data, weights, weights],
            out_specs=pl.BlockSpec(
                (None, None, factor, factor), lambda l, e, lim: (e, l, 0, 0)
            ),
        ),
        compiler_params=pltpu.CompilerParams(vmem_limit_bytes=48 << 20),
        cost_estimate=pl.CostEstimate(flops=flops, transcendentals=0, bytes_accessed=moved),
    )(limits, activations, cotangents, project_in, project_out)


def body_start(activations, cotangents, lengths, project_in, project_out, preconditioner, queries):
    width_mp = lax.axis_size("mp")
    layer_count = activations.shape[0]
    tokens_here = activations.shape[2]
    factor_size = project_in.shape[1]
    block_size = factor_size * factor_size
    group_size = width_mp // layer_count
    mp_place = lax.axis_index("mp")
    contract = (((1,), (1,)), ((), ()))
    positions = mp_place * tokens_here + jnp.arange(tokens_here, dtype=jnp.int32)
    live_mask = positions[None, :] < lengths[:, None]
    left_factor = jnp.einsum(
        "lesd,lkd->lesk", activations, project_in, preferred_element_type=jnp.float32
    ).astype(jnp.bfloat16)
    right_factor = jnp.einsum(
        "lesd,lkd->lesk", cotangents, project_out, preferred_element_type=jnp.float32
    )
    right_factor = jnp.where(live_mask[None, :, :, None], right_factor, 0.0).astype(jnp.bfloat16)
    partial_grad = jnp.einsum(
        "lesj,lesc->eljc", right_factor, left_factor, preferred_element_type=jnp.float32
    )
    partial_grad = partial_grad.reshape(partial_grad.shape[0], layer_count * block_size)
    grad_total = lax.psum(partial_grad, "mp")
    layer_place = mp_place // group_size
    grad_layer = lax.dynamic_slice_in_dim(
        grad_total, layer_place * block_size, block_size, 1
    ).astype(jnp.bfloat16)
    spread = lax.all_to_all(grad_layer, "dp", split_axis=1, concat_axis=0, tiled=True)
    partial_pre = lax.dot_general(
        spread, preconditioner, contract, preferred_element_type=jnp.float32
    )
    precond_grad = lax.psum(partial_pre, "dp")
    upper_grad, lower_grad = split_parts(precond_grad)
    scores = lax.psum_scatter(
        lax.dot_general(queries, upper_grad, contract, preferred_element_type=jnp.float32)
        + lax.dot_general(queries, lower_grad, contract, preferred_element_type=jnp.float32),
        "mp",
        scatter_dimension=0,
        tiled=True,
    )
    return scores.T


def body_direct(activations, cotangents, lengths, project_in, project_out, preconditioner, queries):
    layer_count = activations.shape[0]
    tokens_here = activations.shape[2]
    factor_size = project_in.shape[1]
    block_size = factor_size * factor_size
    width_dp = lax.axis_size("dp")
    mp_place = lax.axis_index("mp")
    limits = lengths - mp_place * tokens_here
    partial_grad = layer_gradients(activations, cotangents, limits, project_in, project_out)
    partial_grad = partial_grad.reshape(partial_grad.shape[0], layer_count * block_size)
    grad_mine = reduce_scatter_direct(partial_grad, "mp", 1).astype(jnp.bfloat16)
    grad_all = all_gather_a2a(grad_mine, "dp")
    grad_all = grad_all.reshape(-1, grad_all.shape[-1])
    pre_part = jnp.dot(grad_all, preconditioner, preferred_element_type=jnp.float32)
    upper_grad, lower_grad = split_parts(pre_part)
    both = jnp.concatenate([upper_grad, lower_grad], axis=0)
    both_all = all_gather_a2a(both, "dp")
    blocks, block = both_all.shape[0], both_all.shape[2]
    query_blocks = queries.reshape(queries.shape[0], blocks, block)
    products = lax.dot_general(
        both_all, query_blocks, (((0, 2), (1, 2)), ((), ())), preferred_element_type=jnp.float32
    )
    examples = upper_grad.shape[0]
    partial_scores = products[:examples] + products[examples:]
    return reduce_scatter_direct(partial_scores, "mp", 1)


def body(*args):
    layer_count = args[0].shape[0]
    if lax.axis_size("mp") == layer_count:
        return body_direct(*args)
    return body_start(*args)


def solution(mesh):
    return jax.shard_map(
        body,
        mesh=mesh,
        in_specs=(
            P(None, "dp", "mp", None),
            P(None, "dp", "mp", None),
            P("dp"),
            P(),
            P(),
            P("mp", "dp"),
            P("dp", "mp"),
        ),
        out_specs=P(None, ("dp", "mp")),
        check_vma=False,
    )
```

```python
import jax
import jax.numpy as jnp
from jax import lax
from jax.experimental import pallas as pl
from jax.experimental.pallas import tpu as pltpu
from jax.sharding import PartitionSpec as P


def split_parts(dense):
    upper = dense.astype(jnp.bfloat16)
    kept = lax.optimization_barrier(upper)
    lower = (dense - kept.astype(jnp.float32)).astype(jnp.bfloat16)
    return (upper, lower)


def shifted(x, axis, shift):
    n = lax.axis_size(axis)
    return lax.ppermute(x, axis, [(i, (i + shift) % n) for i in range(n)])


def reduce_scatter_direct(x, axis, dim):
    n = lax.axis_size(axis)
    me = lax.axis_index(axis)
    width = x.shape[dim] // n
    total = lax.dynamic_slice_in_dim(x, me * width, width, dim)
    for shift in range(1, n):
        piece = lax.dynamic_slice_in_dim(x, ((me + shift) % n) * width, width, dim)
        total = total + shifted(piece, axis, shift)
    return total


def all_gather_direct(x, axis):
    n = lax.axis_size(axis)
    me = lax.axis_index(axis)
    got = [x] + [shifted(x, axis, shift) for shift in range(1, n)]
    order = jnp.stack([got[(-k) % n] for k in range(n)])
    doubled = jnp.concatenate([order, order], axis=0)
    return lax.dynamic_slice_in_dim(doubled, (n - me) % n, n, 0)


def all_gather_a2a(x, axis):
    n = lax.axis_size(axis)
    copies = jnp.broadcast_to(x[None], (n,) + x.shape)
    return lax.all_to_all(copies, axis, 0, 0, tiled=True)


def gradient_kernel(lengths_ref, act_ref, cot_ref, win_ref, wout_ref, out_ref):
    example = pl.program_id(1)
    tokens = act_ref.shape[0]
    limit = lengths_ref[example] - lax.axis_index("mp") * tokens
    nt = (((1,), (1,)), ((), ()))
    left = lax.dot_general(
        act_ref[...], win_ref[...], nt, preferred_element_type=jnp.float32
    ).astype(jnp.bfloat16)
    right = lax.dot_general(cot_ref[...], wout_ref[...], nt, preferred_element_type=jnp.float32)
    rows = lax.broadcasted_iota(jnp.int32, right.shape, 0)
    right = jnp.where(rows < limit, right, 0.0).astype(jnp.bfloat16)
    out_ref[...] = lax.dot_general(
        right, left, (((0,), (0,)), ((), ())), preferred_element_type=jnp.float32
    )


def layer_gradients(activations, cotangents, lengths, project_in, project_out):
    layers, examples, tokens, width = activations.shape
    factor = project_in.shape[1]
    data = pl.BlockSpec((None, None, tokens, width), lambda l, e, lim: (l, e, 0, 0))
    weights = pl.BlockSpec((None, factor, width), lambda l, e, lim: (l, 0, 0))
    flops = 4 * layers * examples * tokens * width * factor
    moved = 2 * (activations.size + cotangents.size + project_in.size + project_out.size)
    return pl.pallas_call(
        gradient_kernel,
        out_shape=jax.ShapeDtypeStruct((examples, layers, factor, factor), jnp.float32),
        grid_spec=pltpu.PrefetchScalarGridSpec(
            num_scalar_prefetch=1,
            grid=(layers, examples),
            in_specs=[data, data, weights, weights],
            out_specs=pl.BlockSpec(
                (None, None, factor, factor), lambda l, e, lim: (e, l, 0, 0)
            ),
        ),
        cost_estimate=pl.CostEstimate(flops=flops, transcendentals=0, bytes_accessed=moved),
    )(lengths, activations, cotangents, project_in, project_out)


def body_start(activations, cotangents, lengths, project_in, project_out, preconditioner, queries):
    width_mp = lax.axis_size("mp")
    layer_count = activations.shape[0]
    tokens_here = activations.shape[2]
    factor_size = project_in.shape[1]
    block_size = factor_size * factor_size
    group_size = width_mp // layer_count
    mp_place = lax.axis_index("mp")
    contract = (((1,), (1,)), ((), ()))
    positions = mp_place * tokens_here + jnp.arange(tokens_here, dtype=jnp.int32)
    live_mask = positions[None, :] < lengths[:, None]
    left_factor = jnp.einsum(
        "lesd,lkd->lesk", activations, project_in, preferred_element_type=jnp.float32
    ).astype(jnp.bfloat16)
    right_factor = jnp.einsum(
        "lesd,lkd->lesk", cotangents, project_out, preferred_element_type=jnp.float32
    )
    right_factor = jnp.where(live_mask[None, :, :, None], right_factor, 0.0).astype(jnp.bfloat16)
    partial_grad = jnp.einsum(
        "lesj,lesc->eljc", right_factor, left_factor, preferred_element_type=jnp.float32
    )
    partial_grad = partial_grad.reshape(partial_grad.shape[0], layer_count * block_size)
    grad_total = lax.psum(partial_grad, "mp")
    layer_place = mp_place // group_size
    grad_layer = lax.dynamic_slice_in_dim(
        grad_total, layer_place * block_size, block_size, 1
    ).astype(jnp.bfloat16)
    spread = lax.all_to_all(grad_layer, "dp", split_axis=1, concat_axis=0, tiled=True)
    partial_pre = lax.dot_general(
        spread, preconditioner, contract, preferred_element_type=jnp.float32
    )
    precond_grad = lax.psum(partial_pre, "dp")
    upper_grad, lower_grad = split_parts(precond_grad)
    scores = lax.psum_scatter(
        lax.dot_general(queries, upper_grad, contract, preferred_element_type=jnp.float32)
        + lax.dot_general(queries, lower_grad, contract, preferred_element_type=jnp.float32),
        "mp",
        scatter_dimension=0,
        tiled=True,
    )
    return scores.T


def body_direct(activations, cotangents, lengths, project_in, project_out, preconditioner, queries):
    layer_count = activations.shape[0]
    tokens_here = activations.shape[2]
    factor_size = project_in.shape[1]
    block_size = factor_size * factor_size
    width_dp = lax.axis_size("dp")
    mp_place = lax.axis_index("mp")
    partial_grad = layer_gradients(activations, cotangents, lengths, project_in, project_out)
    partial_grad = partial_grad.reshape(partial_grad.shape[0], layer_count * block_size)
    grad_mine = reduce_scatter_direct(partial_grad, "mp", 1).astype(jnp.bfloat16)
    grad_all = all_gather_a2a(grad_mine, "dp")
    grad_all = grad_all.reshape(-1, grad_all.shape[-1])
    pre_part = jnp.dot(grad_all, preconditioner, preferred_element_type=jnp.float32)
    upper_grad, lower_grad = split_parts(pre_part)
    both = jnp.concatenate([upper_grad, lower_grad], axis=0)
    both_all = all_gather_a2a(both, "dp")
    blocks, block = both_all.shape[0], both_all.shape[2]
    query_blocks = queries.reshape(queries.shape[0], blocks, block)
    products = lax.dot_general(
        both_all, query_blocks, (((0, 2), (1, 2)), ((), ())), preferred_element_type=jnp.float32
    )
    examples = upper_grad.shape[0]
    partial_scores = products[:examples] + products[examples:]
    return reduce_scatter_direct(partial_scores, "mp", 1)


def body(*args):
    layer_count = args[0].shape[0]
    if lax.axis_size("mp") == layer_count:
        return body_direct(*args)
    return body_start(*args)


def solution(mesh):
    return jax.shard_map(
        body,
        mesh=mesh,
        in_specs=(
            P(None, "dp", "mp", None),
            P(None, "dp", "mp", None),
            P("dp"),
            P(),
            P(),
            P("mp", "dp"),
            P("dp", "mp"),
        ),
        out_specs=P(None, ("dp", "mp")),
        check_vma=False,
    )
```

```python
import jax
import jax.numpy as jnp
from jax import lax
from jax.experimental import pallas as pl
from jax.experimental.pallas import tpu as pltpu
from jax.sharding import PartitionSpec as P


def split_parts(dense):
    upper = dense.astype(jnp.bfloat16)
    kept = lax.optimization_barrier(upper)
    lower = (dense - kept.astype(jnp.float32)).astype(jnp.bfloat16)
    return (upper, lower)


def shifted(x, axis, shift):
    n = lax.axis_size(axis)
    return lax.ppermute(x, axis, [(i, (i + shift) % n) for i in range(n)])


def reduce_scatter_direct(x, axis, dim):
    n = lax.axis_size(axis)
    me = lax.axis_index(axis)
    width = x.shape[dim] // n
    total = lax.dynamic_slice_in_dim(x, me * width, width, dim)
    for shift in range(1, n):
        piece = lax.dynamic_slice_in_dim(x, ((me + shift) % n) * width, width, dim)
        total = total + shifted(piece, axis, shift)
    return total


def all_gather_direct(x, axis):
    n = lax.axis_size(axis)
    me = lax.axis_index(axis)
    got = [x] + [shifted(x, axis, shift) for shift in range(1, n)]
    order = jnp.stack([got[(-k) % n] for k in range(n)])
    doubled = jnp.concatenate([order, order], axis=0)
    return lax.dynamic_slice_in_dim(doubled, (n - me) % n, n, 0)


def all_gather_a2a(x, axis):
    n = lax.axis_size(axis)
    copies = jnp.broadcast_to(x[None], (n,) + x.shape)
    return lax.all_to_all(copies, axis, 0, 0, tiled=True)


def gradient_kernel(layers_ref, lengths_ref, act_ref, cot_ref, win_ref, wout_ref, out_ref):
    example = pl.program_id(1)
    tokens = act_ref.shape[0]
    limit = lengths_ref[example] - lax.axis_index("mp") * tokens
    nt = (((1,), (1,)), ((), ()))
    left = lax.dot_general(
        act_ref[...], win_ref[...], nt, preferred_element_type=jnp.float32
    ).astype(jnp.bfloat16)
    right = lax.dot_general(cot_ref[...], wout_ref[...], nt, preferred_element_type=jnp.float32)
    rows = lax.broadcasted_iota(jnp.int32, right.shape, 0)
    right = jnp.where(rows < limit, right, 0.0).astype(jnp.bfloat16)
    out_ref[...] = lax.dot_general(
        right, left, (((0,), (0,)), ((), ())), preferred_element_type=jnp.float32
    )


def layer_gradients(layers, activations, cotangents, lengths, project_in, project_out):
    slots = layers.shape[0]
    _, examples, tokens, width = activations.shape
    factor = project_in.shape[1]
    data = pl.BlockSpec((None, None, tokens, width), lambda t, e, lay, lens: (lay[t], e, 0, 0))
    weights = pl.BlockSpec((None, factor, width), lambda t, e, lay, lens: (lay[t], 0, 0))
    flops = 4 * slots * examples * tokens * width * factor
    moved = 2 * slots * (examples * tokens * width + factor * width) * 2
    return pl.pallas_call(
        gradient_kernel,
        out_shape=jax.ShapeDtypeStruct((slots, examples, factor, factor), jnp.float32),
        grid_spec=pltpu.PrefetchScalarGridSpec(
            num_scalar_prefetch=2,
            grid=(slots, examples),
            in_specs=[data, data, weights, weights],
            out_specs=pl.BlockSpec(
                (None, None, factor, factor), lambda t, e, lay, lens: (t, e, 0, 0)
            ),
        ),
        cost_estimate=pl.CostEstimate(flops=flops, transcendentals=0, bytes_accessed=moved),
    )(layers, lengths, activations, cotangents, project_in, project_out)


def body_start(activations, cotangents, lengths, project_in, project_out, preconditioner, queries):
    width_mp = lax.axis_size("mp")
    layer_count = activations.shape[0]
    tokens_here = activations.shape[2]
    factor_size = project_in.shape[1]
    block_size = factor_size * factor_size
    group_size = width_mp // layer_count
    mp_place = lax.axis_index("mp")
    contract = (((1,), (1,)), ((), ()))
    positions = mp_place * tokens_here + jnp.arange(tokens_here, dtype=jnp.int32)
    live_mask = positions[None, :] < lengths[:, None]
    left_factor = jnp.einsum(
        "lesd,lkd->lesk", activations, project_in, preferred_element_type=jnp.float32
    ).astype(jnp.bfloat16)
    right_factor = jnp.einsum(
        "lesd,lkd->lesk", cotangents, project_out, preferred_element_type=jnp.float32
    )
    right_factor = jnp.where(live_mask[None, :, :, None], right_factor, 0.0).astype(jnp.bfloat16)
    partial_grad = jnp.einsum(
        "lesj,lesc->eljc", right_factor, left_factor, preferred_element_type=jnp.float32
    )
    partial_grad = partial_grad.reshape(partial_grad.shape[0], layer_count * block_size)
    grad_total = lax.psum(partial_grad, "mp")
    layer_place = mp_place // group_size
    grad_layer = lax.dynamic_slice_in_dim(
        grad_total, layer_place * block_size, block_size, 1
    ).astype(jnp.bfloat16)
    spread = lax.all_to_all(grad_layer, "dp", split_axis=1, concat_axis=0, tiled=True)
    partial_pre = lax.dot_general(
        spread, preconditioner, contract, preferred_element_type=jnp.float32
    )
    precond_grad = lax.psum(partial_pre, "dp")
    upper_grad, lower_grad = split_parts(precond_grad)
    scores = lax.psum_scatter(
        lax.dot_general(queries, upper_grad, contract, preferred_element_type=jnp.float32)
        + lax.dot_general(queries, lower_grad, contract, preferred_element_type=jnp.float32),
        "mp",
        scatter_dimension=0,
        tiled=True,
    )
    return scores.T


def body_direct(activations, cotangents, lengths, project_in, project_out, preconditioner, queries):
    layer_count = activations.shape[0]
    tokens_here = activations.shape[2]
    factor_size = project_in.shape[1]
    block_size = factor_size * factor_size
    width_dp = lax.axis_size("dp")
    mp_place = lax.axis_index("mp")
    others = (mp_place + jnp.arange(1, layer_count, dtype=jnp.int32)) % layer_count
    grad_args = (activations, cotangents, lengths, project_in, project_out)
    grad_others = layer_gradients(others, *grad_args)
    received = [shifted(grad_others[shift - 1], "mp", shift) for shift in range(1, layer_count)]
    grad_mine = layer_gradients(mp_place[None].astype(jnp.int32), *grad_args)[0]
    for grad in received:
        grad_mine = grad_mine + grad
    grad_mine = grad_mine.reshape(grad_mine.shape[0], block_size).astype(jnp.bfloat16)
    grad_all = all_gather_a2a(grad_mine, "dp")
    grad_all = grad_all.reshape(-1, grad_all.shape[-1])
    pre_part = jnp.dot(grad_all, preconditioner, preferred_element_type=jnp.float32)
    upper_grad, lower_grad = split_parts(pre_part)
    both = jnp.concatenate([upper_grad, lower_grad], axis=0)
    both_all = all_gather_a2a(both, "dp")
    blocks, block = both_all.shape[0], both_all.shape[2]
    query_blocks = queries.reshape(queries.shape[0], blocks, block)
    products = lax.dot_general(
        both_all, query_blocks, (((0, 2), (1, 2)), ((), ())), preferred_element_type=jnp.float32
    )
    examples = upper_grad.shape[0]
    partial_scores = products[:examples] + products[examples:]
    return reduce_scatter_direct(partial_scores, "mp", 1)


def body(*args):
    layer_count = args[0].shape[0]
    if lax.axis_size("mp") == layer_count:
        return body_direct(*args)
    return body_start(*args)


def solution(mesh):
    return jax.shard_map(
        body,
        mesh=mesh,
        in_specs=(
            P(None, "dp", "mp", None),
            P(None, "dp", "mp", None),
            P("dp"),
            P(),
            P(),
            P("mp", "dp"),
            P("dp", "mp"),
        ),
        out_specs=P(None, ("dp", "mp")),
        check_vma=False,
    )
```

```python
import jax
import jax.numpy as jnp
from jax import lax
from jax.experimental import pallas as pl
from jax.experimental.pallas import tpu as pltpu
from jax.sharding import PartitionSpec as P


def split_parts(dense):
    upper = dense.astype(jnp.bfloat16)
    kept = lax.optimization_barrier(upper)
    lower = (dense - kept.astype(jnp.float32)).astype(jnp.bfloat16)
    return (upper, lower)


def shifted(x, axis, shift):
    n = lax.axis_size(axis)
    return lax.ppermute(x, axis, [(i, (i + shift) % n) for i in range(n)])


def reduce_scatter_direct(x, axis, dim):
    n = lax.axis_size(axis)
    me = lax.axis_index(axis)
    width = x.shape[dim] // n
    total = lax.dynamic_slice_in_dim(x, me * width, width, dim)
    for shift in range(1, n):
        piece = lax.dynamic_slice_in_dim(x, ((me + shift) % n) * width, width, dim)
        total = total + shifted(piece, axis, shift)
    return total


def all_gather_direct(x, axis):
    n = lax.axis_size(axis)
    me = lax.axis_index(axis)
    got = [x] + [shifted(x, axis, shift) for shift in range(1, n)]
    order = jnp.stack([got[(-k) % n] for k in range(n)])
    doubled = jnp.concatenate([order, order], axis=0)
    return lax.dynamic_slice_in_dim(doubled, (n - me) % n, n, 0)


def all_gather_a2a(x, axis):
    n = lax.axis_size(axis)
    copies = jnp.broadcast_to(x[None], (n,) + x.shape)
    return lax.all_to_all(copies, axis, 0, 0, tiled=True)


def gradient_kernel(lengths_ref, act_ref, cot_ref, win_ref, wout_ref, out_ref):
    example = pl.program_id(1)
    tokens = act_ref.shape[0]
    limit = lengths_ref[example] - lax.axis_index("mp") * tokens
    nt = (((1,), (1,)), ((), ()))
    left = lax.dot_general(
        act_ref[...], win_ref[...], nt, preferred_element_type=jnp.float32
    ).astype(jnp.bfloat16)
    right = lax.dot_general(cot_ref[...], wout_ref[...], nt, preferred_element_type=jnp.float32)
    rows = lax.broadcasted_iota(jnp.int32, right.shape, 0)
    right = jnp.where(rows < limit, right, 0.0).astype(jnp.bfloat16)
    out_ref[...] = lax.dot_general(
        right, left, (((0,), (0,)), ((), ())), preferred_element_type=jnp.float32
    )


def layer_gradients(activations, cotangents, lengths, project_in, project_out):
    layers, examples, tokens, width = activations.shape
    factor = project_in.shape[1]
    data = pl.BlockSpec((None, None, tokens, width), lambda l, e, lim: (l, e, 0, 0))
    weights = pl.BlockSpec((None, factor, width), lambda l, e, lim: (l, 0, 0))
    flops = 4 * layers * examples * tokens * width * factor
    moved = 2 * (activations.size + cotangents.size + project_in.size + project_out.size)
    return pl.pallas_call(
        gradient_kernel,
        out_shape=jax.ShapeDtypeStruct((layers, examples, factor, factor), jnp.float32),
        grid_spec=pltpu.PrefetchScalarGridSpec(
            num_scalar_prefetch=1,
            grid=(layers, examples),
            in_specs=[data, data, weights, weights],
            out_specs=pl.BlockSpec(
                (None, None, factor, factor), lambda l, e, lim: (l, e, 0, 0)
            ),
        ),
        cost_estimate=pl.CostEstimate(flops=flops, transcendentals=0, bytes_accessed=moved),
    )(lengths, activations, cotangents, project_in, project_out)


def body_start(activations, cotangents, lengths, project_in, project_out, preconditioner, queries):
    width_mp = lax.axis_size("mp")
    layer_count = activations.shape[0]
    tokens_here = activations.shape[2]
    factor_size = project_in.shape[1]
    block_size = factor_size * factor_size
    group_size = width_mp // layer_count
    mp_place = lax.axis_index("mp")
    contract = (((1,), (1,)), ((), ()))
    positions = mp_place * tokens_here + jnp.arange(tokens_here, dtype=jnp.int32)
    live_mask = positions[None, :] < lengths[:, None]
    left_factor = jnp.einsum(
        "lesd,lkd->lesk", activations, project_in, preferred_element_type=jnp.float32
    ).astype(jnp.bfloat16)
    right_factor = jnp.einsum(
        "lesd,lkd->lesk", cotangents, project_out, preferred_element_type=jnp.float32
    )
    right_factor = jnp.where(live_mask[None, :, :, None], right_factor, 0.0).astype(jnp.bfloat16)
    partial_grad = jnp.einsum(
        "lesj,lesc->eljc", right_factor, left_factor, preferred_element_type=jnp.float32
    )
    partial_grad = partial_grad.reshape(partial_grad.shape[0], layer_count * block_size)
    grad_total = lax.psum(partial_grad, "mp")
    layer_place = mp_place // group_size
    grad_layer = lax.dynamic_slice_in_dim(
        grad_total, layer_place * block_size, block_size, 1
    ).astype(jnp.bfloat16)
    spread = lax.all_to_all(grad_layer, "dp", split_axis=1, concat_axis=0, tiled=True)
    partial_pre = lax.dot_general(
        spread, preconditioner, contract, preferred_element_type=jnp.float32
    )
    precond_grad = lax.psum(partial_pre, "dp")
    upper_grad, lower_grad = split_parts(precond_grad)
    scores = lax.psum_scatter(
        lax.dot_general(queries, upper_grad, contract, preferred_element_type=jnp.float32)
        + lax.dot_general(queries, lower_grad, contract, preferred_element_type=jnp.float32),
        "mp",
        scatter_dimension=0,
        tiled=True,
    )
    return scores.T


def body_direct(activations, cotangents, lengths, project_in, project_out, preconditioner, queries):
    layer_count = activations.shape[0]
    tokens_here = activations.shape[2]
    factor_size = project_in.shape[1]
    block_size = factor_size * factor_size
    width_dp = lax.axis_size("dp")
    mp_place = lax.axis_index("mp")
    partial_grad = layer_gradients(activations, cotangents, lengths, project_in, project_out)
    grad_mine = reduce_scatter_direct(partial_grad, "mp", 0)[0]
    grad_mine = grad_mine.astype(jnp.bfloat16).reshape(grad_mine.shape[0], block_size)
    grad_all = all_gather_a2a(grad_mine, "dp")
    grad_all = grad_all.reshape(-1, grad_all.shape[-1])
    pre_part = jnp.dot(grad_all, preconditioner, preferred_element_type=jnp.float32)
    upper_grad, lower_grad = split_parts(all_gather_a2a(pre_part, "dp"))
    both_all = jnp.concatenate([upper_grad, lower_grad], axis=1)
    blocks, block = both_all.shape[0], both_all.shape[2]
    query_blocks = queries.reshape(queries.shape[0], blocks, block)
    products = lax.dot_general(
        both_all, query_blocks, (((0, 2), (1, 2)), ((), ())), preferred_element_type=jnp.float32
    )
    examples = upper_grad.shape[1]
    partial_scores = products[:examples] + products[examples:]
    return reduce_scatter_direct(partial_scores, "mp", 1)


def body(*args):
    layer_count = args[0].shape[0]
    if lax.axis_size("mp") == layer_count:
        return body_direct(*args)
    return body_start(*args)


def solution(mesh):
    return jax.shard_map(
        body,
        mesh=mesh,
        in_specs=(
            P(None, "dp", "mp", None),
            P(None, "dp", "mp", None),
            P("dp"),
            P(),
            P(),
            P("mp", "dp"),
            P("dp", "mp"),
        ),
        out_specs=P(None, ("dp", "mp")),
        check_vma=False,
    )
```

```python
import jax
import jax.numpy as jnp
from jax import lax
from jax.experimental import pallas as pl
from jax.experimental.pallas import tpu as pltpu
from jax.sharding import PartitionSpec as P


def split_parts(dense):
    upper = dense.astype(jnp.bfloat16)
    kept = lax.optimization_barrier(upper)
    lower = (dense - kept.astype(jnp.float32)).astype(jnp.bfloat16)
    return (upper, lower)


def shifted(x, axis, shift):
    n = lax.axis_size(axis)
    return lax.ppermute(x, axis, [(i, (i + shift) % n) for i in range(n)])


def reduce_scatter_direct(x, axis, dim):
    n = lax.axis_size(axis)
    me = lax.axis_index(axis)
    width = x.shape[dim] // n
    total = lax.dynamic_slice_in_dim(x, me * width, width, dim)
    for shift in range(1, n):
        piece = lax.dynamic_slice_in_dim(x, ((me + shift) % n) * width, width, dim)
        total = total + shifted(piece, axis, shift)
    return total


def all_gather_direct(x, axis):
    n = lax.axis_size(axis)
    me = lax.axis_index(axis)
    got = [x] + [shifted(x, axis, shift) for shift in range(1, n)]
    order = jnp.stack([got[(-k) % n] for k in range(n)])
    doubled = jnp.concatenate([order, order], axis=0)
    return lax.dynamic_slice_in_dim(doubled, (n - me) % n, n, 0)


def all_gather_a2a(x, axis):
    n = lax.axis_size(axis)
    copies = jnp.broadcast_to(x[None], (n,) + x.shape)
    return lax.all_to_all(copies, axis, 0, 0, tiled=True)


def gradient_kernel(lengths_ref, act_ref, cot_ref, win_ref, wout_ref, out_ref):
    tokens = act_ref.shape[1]
    offset = lax.axis_index("mp") * tokens
    nt = (((1,), (1,)), ((), ()))
    for example in range(act_ref.shape[0]):
        left = lax.dot_general(
            act_ref[example], win_ref[...], nt, preferred_element_type=jnp.float32
        ).astype(jnp.bfloat16)
        right = lax.dot_general(
            cot_ref[example], wout_ref[...], nt, preferred_element_type=jnp.float32
        )
        rows = lax.broadcasted_iota(jnp.int32, right.shape, 0)
        right = jnp.where(rows < lengths_ref[example] - offset, right, 0.0).astype(jnp.bfloat16)
        out_ref[example] = lax.dot_general(
            right, left, (((0,), (0,)), ((), ())), preferred_element_type=jnp.float32
        )


def layer_gradients(activations, cotangents, lengths, project_in, project_out):
    layers, examples, tokens, width = activations.shape
    factor = project_in.shape[1]
    data = pl.BlockSpec((None, examples, tokens, width), lambda l, lens: (l, 0, 0, 0))
    weights = pl.BlockSpec((None, factor, width), lambda l, lens: (l, 0, 0))
    flops = 4 * layers * examples * tokens * width * factor
    moved = 2 * (activations.size + cotangents.size + project_in.size + project_out.size)
    return pl.pallas_call(
        gradient_kernel,
        out_shape=jax.ShapeDtypeStruct((layers, examples, factor, factor), jnp.float32),
        grid_spec=pltpu.PrefetchScalarGridSpec(
            num_scalar_prefetch=1,
            grid=(layers,),
            in_specs=[data, data, weights, weights],
            out_specs=pl.BlockSpec((None, examples, factor, factor), lambda l, lens: (l, 0, 0, 0)),
        ),
        cost_estimate=pl.CostEstimate(flops=flops, transcendentals=0, bytes_accessed=moved),
    )(lengths, activations, cotangents, project_in, project_out)


def body_start(activations, cotangents, lengths, project_in, project_out, preconditioner, queries):
    width_mp = lax.axis_size("mp")
    layer_count = activations.shape[0]
    tokens_here = activations.shape[2]
    factor_size = project_in.shape[1]
    block_size = factor_size * factor_size
    group_size = width_mp // layer_count
    mp_place = lax.axis_index("mp")
    contract = (((1,), (1,)), ((), ()))
    positions = mp_place * tokens_here + jnp.arange(tokens_here, dtype=jnp.int32)
    live_mask = positions[None, :] < lengths[:, None]
    left_factor = jnp.einsum(
        "lesd,lkd->lesk", activations, project_in, preferred_element_type=jnp.float32
    ).astype(jnp.bfloat16)
    right_factor = jnp.einsum(
        "lesd,lkd->lesk", cotangents, project_out, preferred_element_type=jnp.float32
    )
    right_factor = jnp.where(live_mask[None, :, :, None], right_factor, 0.0).astype(jnp.bfloat16)
    partial_grad = jnp.einsum(
        "lesj,lesc->eljc", right_factor, left_factor, preferred_element_type=jnp.float32
    )
    partial_grad = partial_grad.reshape(partial_grad.shape[0], layer_count * block_size)
    grad_total = lax.psum(partial_grad, "mp")
    layer_place = mp_place // group_size
    grad_layer = lax.dynamic_slice_in_dim(
        grad_total, layer_place * block_size, block_size, 1
    ).astype(jnp.bfloat16)
    spread = lax.all_to_all(grad_layer, "dp", split_axis=1, concat_axis=0, tiled=True)
    partial_pre = lax.dot_general(
        spread, preconditioner, contract, preferred_element_type=jnp.float32
    )
    precond_grad = lax.psum(partial_pre, "dp")
    upper_grad, lower_grad = split_parts(precond_grad)
    scores = lax.psum_scatter(
        lax.dot_general(queries, upper_grad, contract, preferred_element_type=jnp.float32)
        + lax.dot_general(queries, lower_grad, contract, preferred_element_type=jnp.float32),
        "mp",
        scatter_dimension=0,
        tiled=True,
    )
    return scores.T


def body_direct(activations, cotangents, lengths, project_in, project_out, preconditioner, queries):
    layer_count = activations.shape[0]
    tokens_here = activations.shape[2]
    factor_size = project_in.shape[1]
    block_size = factor_size * factor_size
    width_dp = lax.axis_size("dp")
    mp_place = lax.axis_index("mp")
    partial_grad = layer_gradients(activations, cotangents, lengths, project_in, project_out)
    grad_mine = reduce_scatter_direct(partial_grad, "mp", 0)[0]
    grad_mine = grad_mine.astype(jnp.bfloat16).reshape(grad_mine.shape[0], block_size)
    grad_all = all_gather_a2a(grad_mine, "dp")
    grad_all = grad_all.reshape(-1, grad_all.shape[-1])
    pre_part = jnp.dot(grad_all, preconditioner, preferred_element_type=jnp.float32)
    upper_grad, lower_grad = split_parts(all_gather_a2a(pre_part, "dp"))
    both_all = jnp.concatenate([upper_grad, lower_grad], axis=1)
    blocks, block = both_all.shape[0], both_all.shape[2]
    query_blocks = queries.reshape(queries.shape[0], blocks, block)
    products = lax.dot_general(
        both_all, query_blocks, (((0, 2), (1, 2)), ((), ())), preferred_element_type=jnp.float32
    )
    examples = upper_grad.shape[1]
    partial_scores = products[:examples] + products[examples:]
    return reduce_scatter_direct(partial_scores, "mp", 1)


def body(*args):
    layer_count = args[0].shape[0]
    if lax.axis_size("mp") == layer_count:
        return body_direct(*args)
    return body_start(*args)


def solution(mesh):
    return jax.shard_map(
        body,
        mesh=mesh,
        in_specs=(
            P(None, "dp", "mp", None),
            P(None, "dp", "mp", None),
            P("dp"),
            P(),
            P(),
            P("mp", "dp"),
            P("dp", "mp"),
        ),
        out_specs=P(None, ("dp", "mp")),
        check_vma=False,
    )
```

```python
import jax
import jax.numpy as jnp
from jax import lax
from jax.experimental import pallas as pl
from jax.experimental.pallas import tpu as pltpu
from jax.sharding import PartitionSpec as P


def split_parts(dense):
    upper = dense.astype(jnp.bfloat16)
    kept = lax.optimization_barrier(upper)
    lower = (dense - kept.astype(jnp.float32)).astype(jnp.bfloat16)
    return (upper, lower)


def shifted(x, axis, shift):
    n = lax.axis_size(axis)
    return lax.ppermute(x, axis, [(i, (i + shift) % n) for i in range(n)])


def reduce_scatter_direct(x, axis, dim):
    n = lax.axis_size(axis)
    me = lax.axis_index(axis)
    width = x.shape[dim] // n
    total = lax.dynamic_slice_in_dim(x, me * width, width, dim)
    for shift in range(1, n):
        piece = lax.dynamic_slice_in_dim(x, ((me + shift) % n) * width, width, dim)
        total = total + shifted(piece, axis, shift)
    return total


def all_gather_direct(x, axis):
    n = lax.axis_size(axis)
    me = lax.axis_index(axis)
    got = [x] + [shifted(x, axis, shift) for shift in range(1, n)]
    order = jnp.stack([got[(-k) % n] for k in range(n)])
    doubled = jnp.concatenate([order, order], axis=0)
    return lax.dynamic_slice_in_dim(doubled, (n - me) % n, n, 0)


def all_gather_a2a(x, axis):
    n = lax.axis_size(axis)
    copies = jnp.broadcast_to(x[None], (n,) + x.shape)
    return lax.all_to_all(copies, axis, 0, 0, tiled=True)


def gradient_kernel(lengths_ref, act_ref, cot_ref, win_ref, wout_ref, out_ref):
    tokens = act_ref.shape[1]
    offset = lax.axis_index("mp") * tokens
    nt = (((1,), (1,)), ((), ()))
    for example in range(act_ref.shape[0]):
        left = lax.dot_general(
            act_ref[example], win_ref[...], nt, preferred_element_type=jnp.float32
        ).astype(jnp.bfloat16)
        right = lax.dot_general(
            cot_ref[example], wout_ref[...], nt, preferred_element_type=jnp.float32
        )
        rows = lax.broadcasted_iota(jnp.int32, right.shape, 0)
        right = jnp.where(rows < lengths_ref[example] - offset, right, 0.0).astype(jnp.bfloat16)
        out_ref[example] = lax.dot_general(
            right, left, (((0,), (0,)), ((), ())), preferred_element_type=jnp.float32
        )


def layer_gradients(activations, cotangents, lengths, project_in, project_out):
    layers, examples, tokens, width = activations.shape
    factor = project_in.shape[1]
    data = pl.BlockSpec((None, examples, tokens, width), lambda l, lens: (l, 0, 0, 0))
    weights = pl.BlockSpec((None, factor, width), lambda l, lens: (l, 0, 0))
    flops = 4 * layers * examples * tokens * width * factor
    moved = 2 * (activations.size + cotangents.size + project_in.size + project_out.size)
    return pl.pallas_call(
        gradient_kernel,
        out_shape=jax.ShapeDtypeStruct((layers, examples, factor, factor), jnp.float32),
        grid_spec=pltpu.PrefetchScalarGridSpec(
            num_scalar_prefetch=1,
            grid=(layers,),
            in_specs=[data, data, weights, weights],
            out_specs=pl.BlockSpec((None, examples, factor, factor), lambda l, lens: (l, 0, 0, 0)),
        ),
        cost_estimate=pl.CostEstimate(flops=flops, transcendentals=0, bytes_accessed=moved),
    )(lengths, activations, cotangents, project_in, project_out)


def scores_kernel(parts_ref, query_ref, out_ref):
    blocks, rows, block = parts_ref.shape
    total = None
    for index in range(blocks):
        term = lax.dot_general(
            parts_ref[index],
            query_ref[:, index * block:(index + 1) * block],
            (((1,), (1,)), ((), ())),
            preferred_element_type=jnp.float32,
        )
        total = term if total is None else total + term
    half = rows // 2
    out_ref[...] = total[:half] + total[half:]


def query_scores(parts, queries):
    blocks, rows, block = parts.shape
    count = queries.shape[0]
    tile = 256 if count % 256 == 0 else count
    flops = 2 * rows * count * blocks * block
    moved = 2 * (parts.size + queries.size) + 4 * (rows // 2) * count
    return pl.pallas_call(
        scores_kernel,
        out_shape=jax.ShapeDtypeStruct((rows // 2, count), jnp.float32),
        grid=(count // tile,),
        in_specs=[
            pl.BlockSpec((blocks, rows, block), lambda i: (0, 0, 0)),
            pl.BlockSpec((tile, queries.shape[1]), lambda i: (i, 0)),
        ],
        out_specs=pl.BlockSpec((rows // 2, tile), lambda i: (0, i)),
        cost_estimate=pl.CostEstimate(flops=flops, transcendentals=0, bytes_accessed=moved),
    )(parts, queries)


def body_start(activations, cotangents, lengths, project_in, project_out, preconditioner, queries):
    width_mp = lax.axis_size("mp")
    layer_count = activations.shape[0]
    tokens_here = activations.shape[2]
    factor_size = project_in.shape[1]
    block_size = factor_size * factor_size
    group_size = width_mp // layer_count
    mp_place = lax.axis_index("mp")
    contract = (((1,), (1,)), ((), ()))
    positions = mp_place * tokens_here + jnp.arange(tokens_here, dtype=jnp.int32)
    live_mask = positions[None, :] < lengths[:, None]
    left_factor = jnp.einsum(
        "lesd,lkd->lesk", activations, project_in, preferred_element_type=jnp.float32
    ).astype(jnp.bfloat16)
    right_factor = jnp.einsum(
        "lesd,lkd->lesk", cotangents, project_out, preferred_element_type=jnp.float32
    )
    right_factor = jnp.where(live_mask[None, :, :, None], right_factor, 0.0).astype(jnp.bfloat16)
    partial_grad = jnp.einsum(
        "lesj,lesc->eljc", right_factor, left_factor, preferred_element_type=jnp.float32
    )
    partial_grad = partial_grad.reshape(partial_grad.shape[0], layer_count * block_size)
    grad_total = lax.psum(partial_grad, "mp")
    layer_place = mp_place // group_size
    grad_layer = lax.dynamic_slice_in_dim(
        grad_total, layer_place * block_size, block_size, 1
    ).astype(jnp.bfloat16)
    spread = lax.all_to_all(grad_layer, "dp", split_axis=1, concat_axis=0, tiled=True)
    partial_pre = lax.dot_general(
        spread, preconditioner, contract, preferred_element_type=jnp.float32
    )
    precond_grad = lax.psum(partial_pre, "dp")
    upper_grad, lower_grad = split_parts(precond_grad)
    scores = lax.psum_scatter(
        lax.dot_general(queries, upper_grad, contract, preferred_element_type=jnp.float32)
        + lax.dot_general(queries, lower_grad, contract, preferred_element_type=jnp.float32),
        "mp",
        scatter_dimension=0,
        tiled=True,
    )
    return scores.T


def body_direct(activations, cotangents, lengths, project_in, project_out, preconditioner, queries):
    layer_count = activations.shape[0]
    tokens_here = activations.shape[2]
    factor_size = project_in.shape[1]
    block_size = factor_size * factor_size
    width_dp = lax.axis_size("dp")
    mp_place = lax.axis_index("mp")
    partial_grad = layer_gradients(activations, cotangents, lengths, project_in, project_out)
    grad_mine = reduce_scatter_direct(partial_grad, "mp", 0)[0]
    grad_mine = grad_mine.astype(jnp.bfloat16).reshape(grad_mine.shape[0], block_size)
    grad_all = all_gather_a2a(grad_mine, "dp")
    grad_all = grad_all.reshape(-1, grad_all.shape[-1])
    pre_part = jnp.dot(grad_all, preconditioner, preferred_element_type=jnp.float32)
    upper_grad, lower_grad = split_parts(all_gather_a2a(pre_part, "dp"))
    both_all = jnp.concatenate([upper_grad, lower_grad], axis=1)
    partial_scores = query_scores(both_all, queries)
    return reduce_scatter_direct(partial_scores, "mp", 1)


def body(*args):
    layer_count = args[0].shape[0]
    if lax.axis_size("mp") == layer_count:
        return body_direct(*args)
    return body_start(*args)


def solution(mesh):
    return jax.shard_map(
        body,
        mesh=mesh,
        in_specs=(
            P(None, "dp", "mp", None),
            P(None, "dp", "mp", None),
            P("dp"),
            P(),
            P(),
            P("mp", "dp"),
            P("dp", "mp"),
        ),
        out_specs=P(None, ("dp", "mp")),
        check_vma=False,
    )
```

```python
import jax
import jax.numpy as jnp
from jax import lax
from jax.experimental import pallas as pl
from jax.experimental.pallas import tpu as pltpu
from jax.sharding import PartitionSpec as P


def split_parts(dense):
    upper = dense.astype(jnp.bfloat16)
    kept = lax.optimization_barrier(upper)
    lower = (dense - kept.astype(jnp.float32)).astype(jnp.bfloat16)
    return (upper, lower)


def shifted(x, axis, shift):
    n = lax.axis_size(axis)
    return lax.ppermute(x, axis, [(i, (i + shift) % n) for i in range(n)])


def reduce_scatter_direct(x, axis, dim):
    n = lax.axis_size(axis)
    me = lax.axis_index(axis)
    width = x.shape[dim] // n
    total = lax.dynamic_slice_in_dim(x, me * width, width, dim)
    for shift in range(1, n):
        piece = lax.dynamic_slice_in_dim(x, ((me + shift) % n) * width, width, dim)
        total = total + shifted(piece, axis, shift)
    return total


def all_gather_direct(x, axis):
    n = lax.axis_size(axis)
    me = lax.axis_index(axis)
    got = [x] + [shifted(x, axis, shift) for shift in range(1, n)]
    order = jnp.stack([got[(-k) % n] for k in range(n)])
    doubled = jnp.concatenate([order, order], axis=0)
    return lax.dynamic_slice_in_dim(doubled, (n - me) % n, n, 0)


def all_gather_a2a(x, axis):
    n = lax.axis_size(axis)
    copies = jnp.broadcast_to(x[None], (n,) + x.shape)
    return lax.all_to_all(copies, axis, 0, 0, tiled=True)


def gradient_kernel(lengths_ref, act_ref, cot_ref, win_ref, wout_ref, out_ref):
    tokens = act_ref.shape[1]
    offset = lax.axis_index("mp") * tokens
    nt = (((1,), (1,)), ((), ()))
    for example in range(act_ref.shape[0]):
        left = lax.dot_general(
            act_ref[example], win_ref[...], nt, preferred_element_type=jnp.float32
        ).astype(jnp.bfloat16)
        right = lax.dot_general(
            cot_ref[example], wout_ref[...], nt, preferred_element_type=jnp.float32
        )
        rows = lax.broadcasted_iota(jnp.int32, right.shape, 0)
        right = jnp.where(rows < lengths_ref[example] - offset, right, 0.0).astype(jnp.bfloat16)
        out_ref[example] = lax.dot_general(
            right, left, (((0,), (0,)), ((), ())), preferred_element_type=jnp.float32
        )


def layer_gradients(activations, cotangents, lengths, project_in, project_out):
    layers, examples, tokens, width = activations.shape
    factor = project_in.shape[1]
    data = pl.BlockSpec((None, examples, tokens, width), lambda l, lens: (l, 0, 0, 0))
    weights = pl.BlockSpec((None, factor, width), lambda l, lens: (l, 0, 0))
    flops = 4 * layers * examples * tokens * width * factor
    moved = 2 * (activations.size + cotangents.size + project_in.size + project_out.size)
    return pl.pallas_call(
        gradient_kernel,
        out_shape=jax.ShapeDtypeStruct((layers, examples, factor, factor), jnp.float32),
        grid_spec=pltpu.PrefetchScalarGridSpec(
            num_scalar_prefetch=1,
            grid=(layers,),
            in_specs=[data, data, weights, weights],
            out_specs=pl.BlockSpec((None, examples, factor, factor), lambda l, lens: (l, 0, 0, 0)),
        ),
        cost_estimate=pl.CostEstimate(flops=flops, transcendentals=0, bytes_accessed=moved),
    )(lengths, activations, cotangents, project_in, project_out)


def scores_kernel(pre_ref, query_ref, out_ref):
    blocks, examples, block = pre_ref.shape
    total = None
    for index in range(blocks):
        dense = pre_ref[index]
        upper = dense.astype(jnp.bfloat16)
        lower = (dense - upper.astype(jnp.float32)).astype(jnp.bfloat16)
        parts = jnp.concatenate([upper, lower], axis=0)
        term = lax.dot_general(
            query_ref[:, index * block:(index + 1) * block],
            parts,
            (((1,), (1,)), ((), ())),
            preferred_element_type=jnp.float32,
        )
        total = term if total is None else total + term
    flipped = total.T
    out_ref[...] = flipped[:examples] + flipped[examples:]


def query_scores(pre_all, queries):
    blocks, examples, block = pre_all.shape
    count = queries.shape[0]
    tile = 256 if count % 256 == 0 else count
    flops = 4 * examples * count * blocks * block
    moved = 4 * pre_all.size + 2 * queries.size + 4 * examples * count
    return pl.pallas_call(
        scores_kernel,
        out_shape=jax.ShapeDtypeStruct((examples, count), jnp.float32),
        grid=(count // tile,),
        in_specs=[
            pl.BlockSpec((blocks, examples, block), lambda i: (0, 0, 0)),
            pl.BlockSpec((tile, queries.shape[1]), lambda i: (i, 0)),
        ],
        out_specs=pl.BlockSpec((examples, tile), lambda i: (0, i)),
        cost_estimate=pl.CostEstimate(flops=flops, transcendentals=0, bytes_accessed=moved),
    )(pre_all, queries)


def body_start(activations, cotangents, lengths, project_in, project_out, preconditioner, queries):
    width_mp = lax.axis_size("mp")
    layer_count = activations.shape[0]
    tokens_here = activations.shape[2]
    factor_size = project_in.shape[1]
    block_size = factor_size * factor_size
    group_size = width_mp // layer_count
    mp_place = lax.axis_index("mp")
    contract = (((1,), (1,)), ((), ()))
    positions = mp_place * tokens_here + jnp.arange(tokens_here, dtype=jnp.int32)
    live_mask = positions[None, :] < lengths[:, None]
    left_factor = jnp.einsum(
        "lesd,lkd->lesk", activations, project_in, preferred_element_type=jnp.float32
    ).astype(jnp.bfloat16)
    right_factor = jnp.einsum(
        "lesd,lkd->lesk", cotangents, project_out, preferred_element_type=jnp.float32
    )
    right_factor = jnp.where(live_mask[None, :, :, None], right_factor, 0.0).astype(jnp.bfloat16)
    partial_grad = jnp.einsum(
        "lesj,lesc->eljc", right_factor, left_factor, preferred_element_type=jnp.float32
    )
    partial_grad = partial_grad.reshape(partial_grad.shape[0], layer_count * block_size)
    grad_total = lax.psum(partial_grad, "mp")
    layer_place = mp_place // group_size
    grad_layer = lax.dynamic_slice_in_dim(
        grad_total, layer_place * block_size, block_size, 1
    ).astype(jnp.bfloat16)
    spread = lax.all_to_all(grad_layer, "dp", split_axis=1, concat_axis=0, tiled=True)
    partial_pre = lax.dot_general(
        spread, preconditioner, contract, preferred_element_type=jnp.float32
    )
    precond_grad = lax.psum(partial_pre, "dp")
    upper_grad, lower_grad = split_parts(precond_grad)
    scores = lax.psum_scatter(
        lax.dot_general(queries, upper_grad, contract, preferred_element_type=jnp.float32)
        + lax.dot_general(queries, lower_grad, contract, preferred_element_type=jnp.float32),
        "mp",
        scatter_dimension=0,
        tiled=True,
    )
    return scores.T


def body_direct(activations, cotangents, lengths, project_in, project_out, preconditioner, queries):
    layer_count = activations.shape[0]
    tokens_here = activations.shape[2]
    factor_size = project_in.shape[1]
    block_size = factor_size * factor_size
    width_dp = lax.axis_size("dp")
    mp_place = lax.axis_index("mp")
    partial_grad = layer_gradients(activations, cotangents, lengths, project_in, project_out)
    grad_mine = reduce_scatter_direct(partial_grad, "mp", 0)[0]
    grad_mine = grad_mine.astype(jnp.bfloat16).reshape(grad_mine.shape[0], block_size)
    grad_all = all_gather_a2a(grad_mine, "dp")
    grad_all = grad_all.reshape(-1, grad_all.shape[-1])
    pre_part = jnp.dot(grad_all, preconditioner, preferred_element_type=jnp.float32)
    partial_scores = query_scores(all_gather_a2a(pre_part, "dp"), queries)
    return reduce_scatter_direct(partial_scores, "mp", 1)


def body(*args):
    layer_count = args[0].shape[0]
    if lax.axis_size("mp") == layer_count:
        return body_direct(*args)
    return body_start(*args)


def solution(mesh):
    return jax.shard_map(
        body,
        mesh=mesh,
        in_specs=(
            P(None, "dp", "mp", None),
            P(None, "dp", "mp", None),
            P("dp"),
            P(),
            P(),
            P("mp", "dp"),
            P("dp", "mp"),
        ),
        out_specs=P(None, ("dp", "mp")),
        check_vma=False,
    )
```

```python
import jax
import jax.numpy as jnp
from jax import lax
from jax.experimental import pallas as pl
from jax.experimental.pallas import tpu as pltpu
from jax.sharding import PartitionSpec as P


def split_parts(dense):
    upper = dense.astype(jnp.bfloat16)
    kept = lax.optimization_barrier(upper)
    lower = (dense - kept.astype(jnp.float32)).astype(jnp.bfloat16)
    return (upper, lower)


def shifted(x, axis, shift):
    n = lax.axis_size(axis)
    return lax.ppermute(x, axis, [(i, (i + shift) % n) for i in range(n)])


def reduce_scatter_direct(x, axis, dim):
    n = lax.axis_size(axis)
    me = lax.axis_index(axis)
    width = x.shape[dim] // n
    total = lax.dynamic_slice_in_dim(x, me * width, width, dim)
    for shift in range(1, n):
        piece = lax.dynamic_slice_in_dim(x, ((me + shift) % n) * width, width, dim)
        total = total + shifted(piece, axis, shift)
    return total


def all_gather_direct(x, axis):
    n = lax.axis_size(axis)
    me = lax.axis_index(axis)
    got = [x] + [shifted(x, axis, shift) for shift in range(1, n)]
    order = jnp.stack([got[(-k) % n] for k in range(n)])
    doubled = jnp.concatenate([order, order], axis=0)
    return lax.dynamic_slice_in_dim(doubled, (n - me) % n, n, 0)


def all_gather_a2a(x, axis):
    n = lax.axis_size(axis)
    copies = jnp.broadcast_to(x[None], (n,) + x.shape)
    return lax.all_to_all(copies, axis, 0, 0, tiled=True)


def gradient_kernel(lengths_ref, act_ref, cot_hbm, win_ref, wout_ref, out_ref, cot_buf, sem):
    layer = pl.program_id(0)
    fetch = pltpu.make_async_copy(cot_hbm.at[layer], cot_buf, sem)
    fetch.start()
    tokens = act_ref.shape[1]
    offset = lax.axis_index("mp") * tokens
    nt = (((1,), (1,)), ((), ()))
    lefts = [
        lax.dot_general(
            act_ref[example], win_ref[...], nt, preferred_element_type=jnp.float32
        ).astype(jnp.bfloat16)
        for example in range(act_ref.shape[0])
    ]
    fetch.wait()
    for example, left in enumerate(lefts):
        right = lax.dot_general(
            cot_buf[example], wout_ref[...], nt, preferred_element_type=jnp.float32
        )
        rows = lax.broadcasted_iota(jnp.int32, right.shape, 0)
        right = jnp.where(rows < lengths_ref[example] - offset, right, 0.0).astype(jnp.bfloat16)
        out_ref[example] = lax.dot_general(
            right, left, (((0,), (0,)), ((), ())), preferred_element_type=jnp.float32
        )


def layer_gradients(activations, cotangents, lengths, project_in, project_out):
    layers, examples, tokens, width = activations.shape
    factor = project_in.shape[1]
    data = pl.BlockSpec((None, examples, tokens, width), lambda l, lens: (l, 0, 0, 0))
    weights = pl.BlockSpec((None, factor, width), lambda l, lens: (l, 0, 0))
    flops = 4 * layers * examples * tokens * width * factor
    moved = 2 * (activations.size + cotangents.size + project_in.size + project_out.size)
    return pl.pallas_call(
        gradient_kernel,
        out_shape=jax.ShapeDtypeStruct((layers, examples, factor, factor), jnp.float32),
        grid_spec=pltpu.PrefetchScalarGridSpec(
            num_scalar_prefetch=1,
            grid=(layers,),
            in_specs=[data, pl.BlockSpec(memory_space=pl.ANY), weights, weights],
            out_specs=pl.BlockSpec((None, examples, factor, factor), lambda l, lens: (l, 0, 0, 0)),
            scratch_shapes=[
                pltpu.VMEM((examples, tokens, width), cotangents.dtype),
                pltpu.SemaphoreType.DMA(()),
            ],
        ),
        cost_estimate=pl.CostEstimate(flops=flops, transcendentals=0, bytes_accessed=moved),
    )(lengths, activations, cotangents, project_in, project_out)


def body_start(activations, cotangents, lengths, project_in, project_out, preconditioner, queries):
    width_mp = lax.axis_size("mp")
    layer_count = activations.shape[0]
    tokens_here = activations.shape[2]
    factor_size = project_in.shape[1]
    block_size = factor_size * factor_size
    group_size = width_mp // layer_count
    mp_place = lax.axis_index("mp")
    contract = (((1,), (1,)), ((), ()))
    positions = mp_place * tokens_here + jnp.arange(tokens_here, dtype=jnp.int32)
    live_mask = positions[None, :] < lengths[:, None]
    left_factor = jnp.einsum(
        "lesd,lkd->lesk", activations, project_in, preferred_element_type=jnp.float32
    ).astype(jnp.bfloat16)
    right_factor = jnp.einsum(
        "lesd,lkd->lesk", cotangents, project_out, preferred_element_type=jnp.float32
    )
    right_factor = jnp.where(live_mask[None, :, :, None], right_factor, 0.0).astype(jnp.bfloat16)
    partial_grad = jnp.einsum(
        "lesj,lesc->eljc", right_factor, left_factor, preferred_element_type=jnp.float32
    )
    partial_grad = partial_grad.reshape(partial_grad.shape[0], layer_count * block_size)
    grad_total = lax.psum(partial_grad, "mp")
    layer_place = mp_place // group_size
    grad_layer = lax.dynamic_slice_in_dim(
        grad_total, layer_place * block_size, block_size, 1
    ).astype(jnp.bfloat16)
    spread = lax.all_to_all(grad_layer, "dp", split_axis=1, concat_axis=0, tiled=True)
    partial_pre = lax.dot_general(
        spread, preconditioner, contract, preferred_element_type=jnp.float32
    )
    precond_grad = lax.psum(partial_pre, "dp")
    upper_grad, lower_grad = split_parts(precond_grad)
    scores = lax.psum_scatter(
        lax.dot_general(queries, upper_grad, contract, preferred_element_type=jnp.float32)
        + lax.dot_general(queries, lower_grad, contract, preferred_element_type=jnp.float32),
        "mp",
        scatter_dimension=0,
        tiled=True,
    )
    return scores.T


def body_direct(activations, cotangents, lengths, project_in, project_out, preconditioner, queries):
    layer_count = activations.shape[0]
    tokens_here = activations.shape[2]
    factor_size = project_in.shape[1]
    block_size = factor_size * factor_size
    width_dp = lax.axis_size("dp")
    mp_place = lax.axis_index("mp")
    partial_grad = layer_gradients(activations, cotangents, lengths, project_in, project_out)
    grad_mine = reduce_scatter_direct(partial_grad, "mp", 0)[0]
    grad_mine = grad_mine.astype(jnp.bfloat16).reshape(grad_mine.shape[0], block_size)
    grad_all = all_gather_a2a(grad_mine, "dp")
    grad_all = grad_all.reshape(-1, grad_all.shape[-1])
    pre_part = jnp.dot(grad_all, preconditioner, preferred_element_type=jnp.float32)
    upper_grad, lower_grad = split_parts(all_gather_a2a(pre_part, "dp"))
    both_all = jnp.concatenate([upper_grad, lower_grad], axis=1)
    blocks, block = both_all.shape[0], both_all.shape[2]
    query_blocks = queries.reshape(queries.shape[0], blocks, block)
    products = lax.dot_general(
        both_all, query_blocks, (((0, 2), (1, 2)), ((), ())), preferred_element_type=jnp.float32
    )
    examples = upper_grad.shape[1]
    partial_scores = products[:examples] + products[examples:]
    return reduce_scatter_direct(partial_scores, "mp", 1)


def body(*args):
    layer_count = args[0].shape[0]
    if lax.axis_size("mp") == layer_count:
        return body_direct(*args)
    return body_start(*args)


def solution(mesh):
    return jax.shard_map(
        body,
        mesh=mesh,
        in_specs=(
            P(None, "dp", "mp", None),
            P(None, "dp", "mp", None),
            P("dp"),
            P(),
            P(),
            P("mp", "dp"),
            P("dp", "mp"),
        ),
        out_specs=P(None, ("dp", "mp")),
        check_vma=False,
    )
```

```python
import jax
import jax.numpy as jnp
from jax import lax
from jax.experimental import pallas as pl
from jax.experimental.pallas import tpu as pltpu
from jax.sharding import PartitionSpec as P


def split_parts(dense):
    upper = dense.astype(jnp.bfloat16)
    kept = lax.optimization_barrier(upper)
    lower = (dense - kept.astype(jnp.float32)).astype(jnp.bfloat16)
    return (upper, lower)


def shifted(x, axis, shift):
    n = lax.axis_size(axis)
    return lax.ppermute(x, axis, [(i, (i + shift) % n) for i in range(n)])


def reduce_scatter_direct(x, axis, dim):
    n = lax.axis_size(axis)
    me = lax.axis_index(axis)
    width = x.shape[dim] // n
    total = lax.dynamic_slice_in_dim(x, me * width, width, dim)
    for shift in range(1, n):
        piece = lax.dynamic_slice_in_dim(x, ((me + shift) % n) * width, width, dim)
        total = total + shifted(piece, axis, shift)
    return total


def all_gather_direct(x, axis):
    n = lax.axis_size(axis)
    me = lax.axis_index(axis)
    got = [x] + [shifted(x, axis, shift) for shift in range(1, n)]
    order = jnp.stack([got[(-k) % n] for k in range(n)])
    doubled = jnp.concatenate([order, order], axis=0)
    return lax.dynamic_slice_in_dim(doubled, (n - me) % n, n, 0)


def all_gather_a2a(x, axis):
    n = lax.axis_size(axis)
    copies = jnp.broadcast_to(x[None], (n,) + x.shape)
    return lax.all_to_all(copies, axis, 0, 0, tiled=True)


def gradient_kernel(order_ref, lengths_ref, act_ref, cot_ref, win_ref, wout_ref, *out_refs):
    step = pl.program_id(0)
    tokens = act_ref.shape[1]
    offset = lax.axis_index("mp") * tokens
    nt = (((1,), (1,)), ((), ()))
    grads = []
    for example in range(act_ref.shape[0]):
        left = lax.dot_general(
            act_ref[example], win_ref[...], nt, preferred_element_type=jnp.float32
        ).astype(jnp.bfloat16)
        right = lax.dot_general(
            cot_ref[example], wout_ref[...], nt, preferred_element_type=jnp.float32
        )
        rows = lax.broadcasted_iota(jnp.int32, right.shape, 0)
        right = jnp.where(rows < lengths_ref[example] - offset, right, 0.0).astype(jnp.bfloat16)
        grads.append(lax.dot_general(
            right, left, (((0,), (0,)), ((), ())), preferred_element_type=jnp.float32
        ))
    for index, out_ref in enumerate(out_refs):
        @pl.when(step == index)
        def _():
            for example, grad in enumerate(grads):
                out_ref[example] = grad


def layer_gradients(order, activations, cotangents, lengths, project_in, project_out):
    layers, examples, tokens, width = activations.shape
    factor = project_in.shape[1]
    data = pl.BlockSpec((None, examples, tokens, width), lambda t, rank, lens: (rank[t], 0, 0, 0))
    weights = pl.BlockSpec((None, factor, width), lambda t, rank, lens: (rank[t], 0, 0))
    result = pl.BlockSpec((examples, factor, factor), lambda t, rank, lens: (0, 0, 0))
    flops = 4 * layers * examples * tokens * width * factor
    moved = 2 * (activations.size + cotangents.size + project_in.size + project_out.size)
    return pl.pallas_call(
        gradient_kernel,
        out_shape=[jax.ShapeDtypeStruct((examples, factor, factor), jnp.float32)] * layers,
        grid_spec=pltpu.PrefetchScalarGridSpec(
            num_scalar_prefetch=2,
            grid=(layers,),
            in_specs=[data, data, weights, weights],
            out_specs=[result] * layers,
        ),
        cost_estimate=pl.CostEstimate(flops=flops, transcendentals=0, bytes_accessed=moved),
    )(order, lengths, activations, cotangents, project_in, project_out)


def body_start(activations, cotangents, lengths, project_in, project_out, preconditioner, queries):
    width_mp = lax.axis_size("mp")
    layer_count = activations.shape[0]
    tokens_here = activations.shape[2]
    factor_size = project_in.shape[1]
    block_size = factor_size * factor_size
    group_size = width_mp // layer_count
    mp_place = lax.axis_index("mp")
    contract = (((1,), (1,)), ((), ()))
    positions = mp_place * tokens_here + jnp.arange(tokens_here, dtype=jnp.int32)
    live_mask = positions[None, :] < lengths[:, None]
    left_factor = jnp.einsum(
        "lesd,lkd->lesk", activations, project_in, preferred_element_type=jnp.float32
    ).astype(jnp.bfloat16)
    right_factor = jnp.einsum(
        "lesd,lkd->lesk", cotangents, project_out, preferred_element_type=jnp.float32
    )
    right_factor = jnp.where(live_mask[None, :, :, None], right_factor, 0.0).astype(jnp.bfloat16)
    partial_grad = jnp.einsum(
        "lesj,lesc->eljc", right_factor, left_factor, preferred_element_type=jnp.float32
    )
    partial_grad = partial_grad.reshape(partial_grad.shape[0], layer_count * block_size)
    grad_total = lax.psum(partial_grad, "mp")
    layer_place = mp_place // group_size
    grad_layer = lax.dynamic_slice_in_dim(
        grad_total, layer_place * block_size, block_size, 1
    ).astype(jnp.bfloat16)
    spread = lax.all_to_all(grad_layer, "dp", split_axis=1, concat_axis=0, tiled=True)
    partial_pre = lax.dot_general(
        spread, preconditioner, contract, preferred_element_type=jnp.float32
    )
    precond_grad = lax.psum(partial_pre, "dp")
    upper_grad, lower_grad = split_parts(precond_grad)
    scores = lax.psum_scatter(
        lax.dot_general(queries, upper_grad, contract, preferred_element_type=jnp.float32)
        + lax.dot_general(queries, lower_grad, contract, preferred_element_type=jnp.float32),
        "mp",
        scatter_dimension=0,
        tiled=True,
    )
    return scores.T


def body_direct(activations, cotangents, lengths, project_in, project_out, preconditioner, queries):
    layer_count = activations.shape[0]
    tokens_here = activations.shape[2]
    factor_size = project_in.shape[1]
    block_size = factor_size * factor_size
    width_dp = lax.axis_size("dp")
    mp_place = lax.axis_index("mp")
    order = (mp_place + jnp.arange(1, layer_count + 1, dtype=jnp.int32)) % layer_count
    grads = layer_gradients(order, activations, cotangents, lengths, project_in, project_out)
    grad_mine = grads[-1]
    for shift in range(1, layer_count):
        grad_mine = grad_mine + shifted(grads[shift - 1], "mp", shift)
    grad_mine = grad_mine.astype(jnp.bfloat16).reshape(grad_mine.shape[0], block_size)
    grad_all = all_gather_a2a(grad_mine, "dp")
    grad_all = grad_all.reshape(-1, grad_all.shape[-1])
    pre_part = jnp.dot(grad_all, preconditioner, preferred_element_type=jnp.float32)
    upper_grad, lower_grad = split_parts(all_gather_a2a(pre_part, "dp"))
    both_all = jnp.concatenate([upper_grad, lower_grad], axis=1)
    blocks, block = both_all.shape[0], both_all.shape[2]
    query_blocks = queries.reshape(queries.shape[0], blocks, block)
    products = lax.dot_general(
        both_all, query_blocks, (((0, 2), (1, 2)), ((), ())), preferred_element_type=jnp.float32
    )
    examples = upper_grad.shape[1]
    partial_scores = products[:examples] + products[examples:]
    return reduce_scatter_direct(partial_scores, "mp", 1)


def body(*args):
    layer_count = args[0].shape[0]
    if lax.axis_size("mp") == layer_count:
        return body_direct(*args)
    return body_start(*args)


def solution(mesh):
    return jax.shard_map(
        body,
        mesh=mesh,
        in_specs=(
            P(None, "dp", "mp", None),
            P(None, "dp", "mp", None),
            P("dp"),
            P(),
            P(),
            P("mp", "dp"),
            P("dp", "mp"),
        ),
        out_specs=P(None, ("dp", "mp")),
        check_vma=False,
    )
```

```python
import jax
import jax.numpy as jnp
from jax import lax
from jax.experimental import pallas as pl
from jax.experimental.pallas import tpu as pltpu
from jax.sharding import PartitionSpec as P


def split_parts(dense):
    upper = dense.astype(jnp.bfloat16)
    kept = lax.optimization_barrier(upper)
    lower = (dense - kept.astype(jnp.float32)).astype(jnp.bfloat16)
    return (upper, lower)


def shifted(x, axis, shift):
    n = lax.axis_size(axis)
    return lax.ppermute(x, axis, [(i, (i + shift) % n) for i in range(n)])


def reduce_scatter_direct(x, axis, dim):
    n = lax.axis_size(axis)
    me = lax.axis_index(axis)
    width = x.shape[dim] // n
    total = lax.dynamic_slice_in_dim(x, me * width, width, dim)
    for shift in range(1, n):
        piece = lax.dynamic_slice_in_dim(x, ((me + shift) % n) * width, width, dim)
        total = total + shifted(piece, axis, shift)
    return total


def all_gather_direct(x, axis):
    n = lax.axis_size(axis)
    me = lax.axis_index(axis)
    got = [x] + [shifted(x, axis, shift) for shift in range(1, n)]
    order = jnp.stack([got[(-k) % n] for k in range(n)])
    doubled = jnp.concatenate([order, order], axis=0)
    return lax.dynamic_slice_in_dim(doubled, (n - me) % n, n, 0)


def all_gather_a2a(x, axis):
    n = lax.axis_size(axis)
    copies = jnp.broadcast_to(x[None], (n,) + x.shape)
    return lax.all_to_all(copies, axis, 0, 0, tiled=True)


def gradient_kernel(lengths_ref, act_ref, cot_ref, win_ref, wout_ref, out_ref, left_acc, right_acc):
    chunk = pl.program_id(1)
    tokens = act_ref.shape[1]
    nt = (((1,), (1,)), ((), ()))
    for example in range(act_ref.shape[0]):
        left = lax.dot_general(
            act_ref[example], win_ref[...], nt, preferred_element_type=jnp.float32
        )
        right = lax.dot_general(
            cot_ref[example], wout_ref[...], nt, preferred_element_type=jnp.float32
        )

        @pl.when(chunk == 0)
        def _():
            left_acc[example] = left
            right_acc[example] = right

        @pl.when(chunk > 0)
        def _():
            left_acc[example] += left
            right_acc[example] += right

    @pl.when(chunk == pl.num_programs(1) - 1)
    def _():
        offset = lax.axis_index("mp") * tokens
        for example in range(act_ref.shape[0]):
            left = left_acc[example].astype(jnp.bfloat16)
            right = right_acc[example]
            rows = lax.broadcasted_iota(jnp.int32, right.shape, 0)
            right = jnp.where(rows < lengths_ref[example] - offset, right, 0.0).astype(jnp.bfloat16)
            out_ref[example] = lax.dot_general(
                right, left, (((0,), (0,)), ((), ())), preferred_element_type=jnp.float32
            )


def layer_gradients(activations, cotangents, lengths, project_in, project_out):
    layers, examples, tokens, width = activations.shape
    factor = project_in.shape[1]
    chunks = 4 if width % 512 == 0 else 1
    part = width // chunks
    data = pl.BlockSpec((None, examples, tokens, part), lambda l, k, lens: (l, 0, 0, k))
    weights = pl.BlockSpec((None, factor, part), lambda l, k, lens: (l, 0, k))
    flops = 4 * layers * examples * tokens * width * factor
    moved = 2 * (activations.size + cotangents.size + project_in.size + project_out.size)
    return pl.pallas_call(
        gradient_kernel,
        out_shape=jax.ShapeDtypeStruct((layers, examples, factor, factor), jnp.float32),
        grid_spec=pltpu.PrefetchScalarGridSpec(
            num_scalar_prefetch=1,
            grid=(layers, chunks),
            in_specs=[data, data, weights, weights],
            out_specs=pl.BlockSpec(
                (None, examples, factor, factor), lambda l, k, lens: (l, 0, 0, 0)
            ),
            scratch_shapes=[
                pltpu.VMEM((examples, tokens, factor), jnp.float32),
                pltpu.VMEM((examples, tokens, factor), jnp.float32),
            ],
        ),
        cost_estimate=pl.CostEstimate(flops=flops, transcendentals=0, bytes_accessed=moved),
    )(lengths, activations, cotangents, project_in, project_out)


def body_start(activations, cotangents, lengths, project_in, project_out, preconditioner, queries):
    width_mp = lax.axis_size("mp")
    layer_count = activations.shape[0]
    tokens_here = activations.shape[2]
    factor_size = project_in.shape[1]
    block_size = factor_size * factor_size
    group_size = width_mp // layer_count
    mp_place = lax.axis_index("mp")
    contract = (((1,), (1,)), ((), ()))
    positions = mp_place * tokens_here + jnp.arange(tokens_here, dtype=jnp.int32)
    live_mask = positions[None, :] < lengths[:, None]
    left_factor = jnp.einsum(
        "lesd,lkd->lesk", activations, project_in, preferred_element_type=jnp.float32
    ).astype(jnp.bfloat16)
    right_factor = jnp.einsum(
        "lesd,lkd->lesk", cotangents, project_out, preferred_element_type=jnp.float32
    )
    right_factor = jnp.where(live_mask[None, :, :, None], right_factor, 0.0).astype(jnp.bfloat16)
    partial_grad = jnp.einsum(
        "lesj,lesc->eljc", right_factor, left_factor, preferred_element_type=jnp.float32
    )
    partial_grad = partial_grad.reshape(partial_grad.shape[0], layer_count * block_size)
    grad_total = lax.psum(partial_grad, "mp")
    layer_place = mp_place // group_size
    grad_layer = lax.dynamic_slice_in_dim(
        grad_total, layer_place * block_size, block_size, 1
    ).astype(jnp.bfloat16)
    spread = lax.all_to_all(grad_layer, "dp", split_axis=1, concat_axis=0, tiled=True)
    partial_pre = lax.dot_general(
        spread, preconditioner, contract, preferred_element_type=jnp.float32
    )
    precond_grad = lax.psum(partial_pre, "dp")
    upper_grad, lower_grad = split_parts(precond_grad)
    scores = lax.psum_scatter(
        lax.dot_general(queries, upper_grad, contract, preferred_element_type=jnp.float32)
        + lax.dot_general(queries, lower_grad, contract, preferred_element_type=jnp.float32),
        "mp",
        scatter_dimension=0,
        tiled=True,
    )
    return scores.T


def body_direct(activations, cotangents, lengths, project_in, project_out, preconditioner, queries):
    layer_count = activations.shape[0]
    tokens_here = activations.shape[2]
    factor_size = project_in.shape[1]
    block_size = factor_size * factor_size
    width_dp = lax.axis_size("dp")
    mp_place = lax.axis_index("mp")
    partial_grad = layer_gradients(activations, cotangents, lengths, project_in, project_out)
    grad_mine = reduce_scatter_direct(partial_grad, "mp", 0)[0]
    grad_mine = grad_mine.astype(jnp.bfloat16).reshape(grad_mine.shape[0], block_size)
    grad_all = all_gather_a2a(grad_mine, "dp")
    grad_all = grad_all.reshape(-1, grad_all.shape[-1])
    pre_part = jnp.dot(grad_all, preconditioner, preferred_element_type=jnp.float32)
    upper_grad, lower_grad = split_parts(all_gather_a2a(pre_part, "dp"))
    both_all = jnp.concatenate([upper_grad, lower_grad], axis=1)
    blocks, block = both_all.shape[0], both_all.shape[2]
    query_blocks = queries.reshape(queries.shape[0], blocks, block)
    products = lax.dot_general(
        both_all, query_blocks, (((0, 2), (1, 2)), ((), ())), preferred_element_type=jnp.float32
    )
    examples = upper_grad.shape[1]
    partial_scores = products[:examples] + products[examples:]
    return reduce_scatter_direct(partial_scores, "mp", 1)


def body(*args):
    layer_count = args[0].shape[0]
    if lax.axis_size("mp") == layer_count:
        return body_direct(*args)
    return body_start(*args)


def solution(mesh):
    return jax.shard_map(
        body,
        mesh=mesh,
        in_specs=(
            P(None, "dp", "mp", None),
            P(None, "dp", "mp", None),
            P("dp"),
            P(),
            P(),
            P("mp", "dp"),
            P("dp", "mp"),
        ),
        out_specs=P(None, ("dp", "mp")),
        check_vma=False,
    )
```

```python
import jax
import jax.numpy as jnp
from jax import lax
from jax.experimental import pallas as pl
from jax.experimental.pallas import tpu as pltpu
from jax.sharding import PartitionSpec as P


def split_parts(dense):
    upper = dense.astype(jnp.bfloat16)
    kept = lax.optimization_barrier(upper)
    lower = (dense - kept.astype(jnp.float32)).astype(jnp.bfloat16)
    return (upper, lower)


def shifted(x, axis, shift):
    n = lax.axis_size(axis)
    return lax.ppermute(x, axis, [(i, (i + shift) % n) for i in range(n)])


def reduce_scatter_direct(x, axis, dim):
    n = lax.axis_size(axis)
    me = lax.axis_index(axis)
    width = x.shape[dim] // n
    total = lax.dynamic_slice_in_dim(x, me * width, width, dim)
    for shift in range(1, n):
        piece = lax.dynamic_slice_in_dim(x, ((me + shift) % n) * width, width, dim)
        total = total + shifted(piece, axis, shift)
    return total


def all_gather_direct(x, axis):
    n = lax.axis_size(axis)
    me = lax.axis_index(axis)
    got = [x] + [shifted(x, axis, shift) for shift in range(1, n)]
    order = jnp.stack([got[(-k) % n] for k in range(n)])
    doubled = jnp.concatenate([order, order], axis=0)
    return lax.dynamic_slice_in_dim(doubled, (n - me) % n, n, 0)


def all_gather_a2a(x, axis):
    n = lax.axis_size(axis)
    copies = jnp.broadcast_to(x[None], (n,) + x.shape)
    return lax.all_to_all(copies, axis, 0, 0, tiled=True)


def gradient_kernel(lengths_ref, act_ref, cot_ref, win_ref, wout_ref, out_ref):
    tokens = act_ref.shape[1]
    offset = lax.axis_index("mp") * tokens
    nt = (((1,), (1,)), ((), ()))
    for example in range(act_ref.shape[0]):
        left = lax.dot_general(
            act_ref[example], win_ref[...], nt, preferred_element_type=jnp.float32
        ).astype(jnp.bfloat16)
        right = lax.dot_general(
            cot_ref[example], wout_ref[...], nt, preferred_element_type=jnp.float32
        )
        rows = lax.broadcasted_iota(jnp.int32, right.shape, 0)
        right = jnp.where(rows < lengths_ref[example] - offset, right, 0.0).astype(jnp.bfloat16)
        out_ref[example] = lax.dot_general(
            right, left, (((0,), (0,)), ((), ())), preferred_element_type=jnp.float32
        )


def layer_gradients(activations, cotangents, lengths, project_in, project_out):
    layers, examples, tokens, width = activations.shape
    factor = project_in.shape[1]
    data = pl.BlockSpec((None, examples, tokens, width), lambda l, lens: (l, 0, 0, 0))
    weights = pl.BlockSpec((None, factor, width), lambda l, lens: (l, 0, 0))
    flops = 4 * layers * examples * tokens * width * factor
    moved = 2 * (activations.size + cotangents.size + project_in.size + project_out.size)
    return pl.pallas_call(
        gradient_kernel,
        out_shape=jax.ShapeDtypeStruct((layers, examples, factor, factor), jnp.float32),
        grid_spec=pltpu.PrefetchScalarGridSpec(
            num_scalar_prefetch=1,
            grid=(layers,),
            in_specs=[data, data, weights, weights],
            out_specs=pl.BlockSpec((None, examples, factor, factor), lambda l, lens: (l, 0, 0, 0)),
        ),
        cost_estimate=pl.CostEstimate(flops=flops, transcendentals=0, bytes_accessed=moved),
    )(lengths, activations, cotangents, project_in, project_out)


def body_start(activations, cotangents, lengths, project_in, project_out, preconditioner, queries):
    width_mp = lax.axis_size("mp")
    layer_count = activations.shape[0]
    tokens_here = activations.shape[2]
    factor_size = project_in.shape[1]
    block_size = factor_size * factor_size
    group_size = width_mp // layer_count
    mp_place = lax.axis_index("mp")
    contract = (((1,), (1,)), ((), ()))
    positions = mp_place * tokens_here + jnp.arange(tokens_here, dtype=jnp.int32)
    live_mask = positions[None, :] < lengths[:, None]
    left_factor = jnp.einsum(
        "lesd,lkd->lesk", activations, project_in, preferred_element_type=jnp.float32
    ).astype(jnp.bfloat16)
    right_factor = jnp.einsum(
        "lesd,lkd->lesk", cotangents, project_out, preferred_element_type=jnp.float32
    )
    right_factor = jnp.where(live_mask[None, :, :, None], right_factor, 0.0).astype(jnp.bfloat16)
    partial_grad = jnp.einsum(
        "lesj,lesc->eljc", right_factor, left_factor, preferred_element_type=jnp.float32
    )
    partial_grad = partial_grad.reshape(partial_grad.shape[0], layer_count * block_size)
    grad_total = lax.psum(partial_grad, "mp")
    layer_place = mp_place // group_size
    grad_layer = lax.dynamic_slice_in_dim(
        grad_total, layer_place * block_size, block_size, 1
    ).astype(jnp.bfloat16)
    spread = lax.all_to_all(grad_layer, "dp", split_axis=1, concat_axis=0, tiled=True)
    partial_pre = lax.dot_general(
        spread, preconditioner, contract, preferred_element_type=jnp.float32
    )
    precond_grad = lax.psum(partial_pre, "dp")
    upper_grad, lower_grad = split_parts(precond_grad)
    scores = lax.psum_scatter(
        lax.dot_general(queries, upper_grad, contract, preferred_element_type=jnp.float32)
        + lax.dot_general(queries, lower_grad, contract, preferred_element_type=jnp.float32),
        "mp",
        scatter_dimension=0,
        tiled=True,
    )
    return scores.T


def body_direct(activations, cotangents, lengths, project_in, project_out, preconditioner, queries):
    layer_count = activations.shape[0]
    tokens_here = activations.shape[2]
    factor_size = project_in.shape[1]
    block_size = factor_size * factor_size
    width_dp = lax.axis_size("dp")
    mp_place = lax.axis_index("mp")
    partial_grad = layer_gradients(activations, cotangents, lengths, project_in, project_out)
    grad_mine = jnp.sum(lax.all_to_all(partial_grad, "mp", 0, 0, tiled=True), axis=0)
    grad_mine = grad_mine.astype(jnp.bfloat16).reshape(grad_mine.shape[0], block_size)
    grad_all = all_gather_a2a(grad_mine, "dp")
    grad_all = grad_all.reshape(-1, grad_all.shape[-1])
    pre_part = jnp.dot(grad_all, preconditioner, preferred_element_type=jnp.float32)
    upper_grad, lower_grad = split_parts(all_gather_a2a(pre_part, "dp"))
    both_all = jnp.concatenate([upper_grad, lower_grad], axis=1)
    blocks, block = both_all.shape[0], both_all.shape[2]
    query_blocks = queries.reshape(queries.shape[0], blocks, block)
    products = lax.dot_general(
        both_all, query_blocks, (((0, 2), (1, 2)), ((), ())), preferred_element_type=jnp.float32
    )
    examples = upper_grad.shape[1]
    partial_scores = products[:examples] + products[examples:]
    return reduce_scatter_direct(partial_scores, "mp", 1)


def body(*args):
    layer_count = args[0].shape[0]
    if lax.axis_size("mp") == layer_count:
        return body_direct(*args)
    return body_start(*args)


def solution(mesh):
    return jax.shard_map(
        body,
        mesh=mesh,
        in_specs=(
            P(None, "dp", "mp", None),
            P(None, "dp", "mp", None),
            P("dp"),
            P(),
            P(),
            P("mp", "dp"),
            P("dp", "mp"),
        ),
        out_specs=P(None, ("dp", "mp")),
        check_vma=False,
    )
```

```python
import jax
import jax.numpy as jnp
from jax import lax
from jax.experimental import pallas as pl
from jax.experimental.pallas import tpu as pltpu
from jax.sharding import PartitionSpec as P


def split_parts(dense):
    upper = dense.astype(jnp.bfloat16)
    kept = lax.optimization_barrier(upper)
    lower = (dense - kept.astype(jnp.float32)).astype(jnp.bfloat16)
    return (upper, lower)


def shifted(x, axis, shift):
    n = lax.axis_size(axis)
    return lax.ppermute(x, axis, [(i, (i + shift) % n) for i in range(n)])


def reduce_scatter_direct(x, axis, dim):
    n = lax.axis_size(axis)
    me = lax.axis_index(axis)
    width = x.shape[dim] // n
    total = lax.dynamic_slice_in_dim(x, me * width, width, dim)
    for shift in range(1, n):
        piece = lax.dynamic_slice_in_dim(x, ((me + shift) % n) * width, width, dim)
        total = total + shifted(piece, axis, shift)
    return total


def all_gather_direct(x, axis):
    n = lax.axis_size(axis)
    me = lax.axis_index(axis)
    got = [x] + [shifted(x, axis, shift) for shift in range(1, n)]
    order = jnp.stack([got[(-k) % n] for k in range(n)])
    doubled = jnp.concatenate([order, order], axis=0)
    return lax.dynamic_slice_in_dim(doubled, (n - me) % n, n, 0)


def all_gather_a2a(x, axis):
    n = lax.axis_size(axis)
    copies = jnp.broadcast_to(x[None], (n,) + x.shape)
    return lax.all_to_all(copies, axis, 0, 0, tiled=True)


def gradient_kernel(lengths_ref, act_ref, cot_ref, win_ref, wout_ref, out_ref):
    examples, tokens, width = act_ref.shape
    offset = lax.axis_index("mp") * tokens
    nt = (((1,), (1,)), ((), ()))
    left = lax.dot_general(
        act_ref[...].reshape(examples * tokens, width), win_ref[...], nt,
        preferred_element_type=jnp.float32,
    ).astype(jnp.bfloat16)
    right = lax.dot_general(
        cot_ref[...].reshape(examples * tokens, width), wout_ref[...], nt,
        preferred_element_type=jnp.float32,
    )
    rows = lax.broadcasted_iota(jnp.int32, (tokens, right.shape[1]), 0)
    for example in range(examples):
        rows_here = slice(example * tokens, (example + 1) * tokens)
        right_here = jnp.where(rows < lengths_ref[example] - offset, right[rows_here], 0.0)
        out_ref[example] = lax.dot_general(
            right_here.astype(jnp.bfloat16), left[rows_here], (((0,), (0,)), ((), ())),
            preferred_element_type=jnp.float32,
        )


def layer_gradients(activations, cotangents, lengths, project_in, project_out):
    layers, examples, tokens, width = activations.shape
    factor = project_in.shape[1]
    data = pl.BlockSpec((None, examples, tokens, width), lambda l, lens: (l, 0, 0, 0))
    weights = pl.BlockSpec((None, factor, width), lambda l, lens: (l, 0, 0))
    flops = 4 * layers * examples * tokens * width * factor
    moved = 2 * (activations.size + cotangents.size + project_in.size + project_out.size)
    return pl.pallas_call(
        gradient_kernel,
        out_shape=jax.ShapeDtypeStruct((layers, examples, factor, factor), jnp.float32),
        grid_spec=pltpu.PrefetchScalarGridSpec(
            num_scalar_prefetch=1,
            grid=(layers,),
            in_specs=[data, data, weights, weights],
            out_specs=pl.BlockSpec((None, examples, factor, factor), lambda l, lens: (l, 0, 0, 0)),
        ),
        cost_estimate=pl.CostEstimate(flops=flops, transcendentals=0, bytes_accessed=moved),
    )(lengths, activations, cotangents, project_in, project_out)


def body_start(activations, cotangents, lengths, project_in, project_out, preconditioner, queries):
    width_mp = lax.axis_size("mp")
    layer_count = activations.shape[0]
    tokens_here = activations.shape[2]
    factor_size = project_in.shape[1]
    block_size = factor_size * factor_size
    group_size = width_mp // layer_count
    mp_place = lax.axis_index("mp")
    contract = (((1,), (1,)), ((), ()))
    positions = mp_place * tokens_here + jnp.arange(tokens_here, dtype=jnp.int32)
    live_mask = positions[None, :] < lengths[:, None]
    left_factor = jnp.einsum(
        "lesd,lkd->lesk", activations, project_in, preferred_element_type=jnp.float32
    ).astype(jnp.bfloat16)
    right_factor = jnp.einsum(
        "lesd,lkd->lesk", cotangents, project_out, preferred_element_type=jnp.float32
    )
    right_factor = jnp.where(live_mask[None, :, :, None], right_factor, 0.0).astype(jnp.bfloat16)
    partial_grad = jnp.einsum(
        "lesj,lesc->eljc", right_factor, left_factor, preferred_element_type=jnp.float32
    )
    partial_grad = partial_grad.reshape(partial_grad.shape[0], layer_count * block_size)
    grad_total = lax.psum(partial_grad, "mp")
    layer_place = mp_place // group_size
    grad_layer = lax.dynamic_slice_in_dim(
        grad_total, layer_place * block_size, block_size, 1
    ).astype(jnp.bfloat16)
    spread = lax.all_to_all(grad_layer, "dp", split_axis=1, concat_axis=0, tiled=True)
    partial_pre = lax.dot_general(
        spread, preconditioner, contract, preferred_element_type=jnp.float32
    )
    precond_grad = lax.psum(partial_pre, "dp")
    upper_grad, lower_grad = split_parts(precond_grad)
    scores = lax.psum_scatter(
        lax.dot_general(queries, upper_grad, contract, preferred_element_type=jnp.float32)
        + lax.dot_general(queries, lower_grad, contract, preferred_element_type=jnp.float32),
        "mp",
        scatter_dimension=0,
        tiled=True,
    )
    return scores.T


def body_direct(activations, cotangents, lengths, project_in, project_out, preconditioner, queries):
    layer_count = activations.shape[0]
    tokens_here = activations.shape[2]
    factor_size = project_in.shape[1]
    block_size = factor_size * factor_size
    width_dp = lax.axis_size("dp")
    mp_place = lax.axis_index("mp")
    partial_grad = layer_gradients(activations, cotangents, lengths, project_in, project_out)
    grad_mine = reduce_scatter_direct(partial_grad, "mp", 0)[0]
    grad_mine = grad_mine.astype(jnp.bfloat16).reshape(grad_mine.shape[0], block_size)
    grad_all = all_gather_a2a(grad_mine, "dp")
    grad_all = grad_all.reshape(-1, grad_all.shape[-1])
    pre_part = jnp.dot(grad_all, preconditioner, preferred_element_type=jnp.float32)
    upper_grad, lower_grad = split_parts(all_gather_a2a(pre_part, "dp"))
    both_all = jnp.concatenate([upper_grad, lower_grad], axis=1)
    blocks, block = both_all.shape[0], both_all.shape[2]
    query_blocks = queries.reshape(queries.shape[0], blocks, block)
    products = lax.dot_general(
        both_all, query_blocks, (((0, 2), (1, 2)), ((), ())), preferred_element_type=jnp.float32
    )
    examples = upper_grad.shape[1]
    partial_scores = products[:examples] + products[examples:]
    return reduce_scatter_direct(partial_scores, "mp", 1)


def body(*args):
    layer_count = args[0].shape[0]
    if lax.axis_size("mp") == layer_count:
        return body_direct(*args)
    return body_start(*args)


def solution(mesh):
    return jax.shard_map(
        body,
        mesh=mesh,
        in_specs=(
            P(None, "dp", "mp", None),
            P(None, "dp", "mp", None),
            P("dp"),
            P(),
            P(),
            P("mp", "dp"),
            P("dp", "mp"),
        ),
        out_specs=P(None, ("dp", "mp")),
        check_vma=False,
    )
```

```python
import jax
import jax.numpy as jnp
from jax import lax
from jax.experimental import pallas as pl
from jax.experimental.pallas import tpu as pltpu
from jax.sharding import PartitionSpec as P


def split_parts(dense):
    upper = dense.astype(jnp.bfloat16)
    kept = lax.optimization_barrier(upper)
    lower = (dense - kept.astype(jnp.float32)).astype(jnp.bfloat16)
    return (upper, lower)


def shifted(x, axis, shift):
    n = lax.axis_size(axis)
    return lax.ppermute(x, axis, [(i, (i + shift) % n) for i in range(n)])


def reduce_scatter_direct(x, axis, dim):
    n = lax.axis_size(axis)
    me = lax.axis_index(axis)
    width = x.shape[dim] // n
    total = lax.dynamic_slice_in_dim(x, me * width, width, dim)
    for shift in range(1, n):
        piece = lax.dynamic_slice_in_dim(x, ((me + shift) % n) * width, width, dim)
        total = total + shifted(piece, axis, shift)
    return total


def all_gather_direct(x, axis):
    n = lax.axis_size(axis)
    me = lax.axis_index(axis)
    got = [x] + [shifted(x, axis, shift) for shift in range(1, n)]
    order = jnp.stack([got[(-k) % n] for k in range(n)])
    doubled = jnp.concatenate([order, order], axis=0)
    return lax.dynamic_slice_in_dim(doubled, (n - me) % n, n, 0)


def all_gather_a2a(x, axis):
    n = lax.axis_size(axis)
    copies = jnp.broadcast_to(x[None], (n,) + x.shape)
    return lax.all_to_all(copies, axis, 0, 0, tiled=True)


def gradient_kernel(lengths_ref, act_ref, cot_ref, win_ref, wout_ref, out_ref):
    examples, tokens, width = act_ref.shape
    offset = lax.axis_index("mp") * tokens
    nt = (((1,), (1,)), ((), ()))
    left = lax.dot_general(
        act_ref[...].reshape(examples * tokens, width), win_ref[...], nt,
        preferred_element_type=jnp.float32,
    ).astype(jnp.bfloat16)
    right = lax.dot_general(
        cot_ref[...].reshape(examples * tokens, width), wout_ref[...], nt,
        preferred_element_type=jnp.float32,
    )
    rows = lax.broadcasted_iota(jnp.int32, (tokens, right.shape[1]), 0)
    for example in range(examples):
        rows_here = slice(example * tokens, (example + 1) * tokens)
        right_here = jnp.where(rows < lengths_ref[example] - offset, right[rows_here], 0.0)
        out_ref[example] = lax.dot_general(
            right_here.astype(jnp.bfloat16), left[rows_here], (((0,), (0,)), ((), ())),
            preferred_element_type=jnp.float32,
        )


def layer_gradients(activations, cotangents, lengths, project_in, project_out):
    layers, examples, tokens, width = activations.shape
    factor = project_in.shape[1]
    data = pl.BlockSpec((None, examples, tokens, width), lambda l, lens: (l, 0, 0, 0))
    weights = pl.BlockSpec((None, factor, width), lambda l, lens: (l, 0, 0))
    flops = 4 * layers * examples * tokens * width * factor
    moved = 2 * (activations.size + cotangents.size + project_in.size + project_out.size)
    return pl.pallas_call(
        gradient_kernel,
        out_shape=jax.ShapeDtypeStruct((layers, examples, factor, factor), jnp.float32),
        grid_spec=pltpu.PrefetchScalarGridSpec(
            num_scalar_prefetch=1,
            grid=(layers,),
            in_specs=[data, data, weights, weights],
            out_specs=pl.BlockSpec((None, examples, factor, factor), lambda l, lens: (l, 0, 0, 0)),
        ),
        cost_estimate=pl.CostEstimate(flops=flops, transcendentals=0, bytes_accessed=moved),
    )(lengths, activations, cotangents, project_in, project_out)


def precondition_kernel(grad_ref, block_ref, out_ref, total_ref):
    chunk = pl.program_id(0)
    term = jnp.dot(grad_ref[...], block_ref[...], preferred_element_type=jnp.float32)

    @pl.when(chunk == 0)
    def _():
        total_ref[...] = term

    @pl.when(chunk > 0)
    def _():
        total_ref[...] += term

    @pl.when(chunk == pl.num_programs(0) - 1)
    def _():
        for copy in range(out_ref.shape[0]):
            out_ref[copy] = total_ref[...]


def precondition(grad_all, preconditioner, copies):
    rows, depth = grad_all.shape
    width = preconditioner.shape[1]
    chunks = 4 if depth % 512 == 0 else 1
    part = depth // chunks
    return pl.pallas_call(
        precondition_kernel,
        out_shape=jax.ShapeDtypeStruct((copies, rows, width), jnp.float32),
        grid=(chunks,),
        in_specs=[
            pl.BlockSpec((rows, part), lambda k: (0, k)),
            pl.BlockSpec((part, width), lambda k: (k, 0)),
        ],
        out_specs=pl.BlockSpec((copies, rows, width), lambda k: (0, 0, 0)),
        scratch_shapes=[pltpu.VMEM((rows, width), jnp.float32)],
        cost_estimate=pl.CostEstimate(
            flops=2 * rows * depth * width,
            transcendentals=0,
            bytes_accessed=2 * (grad_all.size + preconditioner.size) + 4 * copies * rows * width,
        ),
    )(grad_all, preconditioner)


def body_start(activations, cotangents, lengths, project_in, project_out, preconditioner, queries):
    width_mp = lax.axis_size("mp")
    layer_count = activations.shape[0]
    tokens_here = activations.shape[2]
    factor_size = project_in.shape[1]
    block_size = factor_size * factor_size
    group_size = width_mp // layer_count
    mp_place = lax.axis_index("mp")
    contract = (((1,), (1,)), ((), ()))
    positions = mp_place * tokens_here + jnp.arange(tokens_here, dtype=jnp.int32)
    live_mask = positions[None, :] < lengths[:, None]
    left_factor = jnp.einsum(
        "lesd,lkd->lesk", activations, project_in, preferred_element_type=jnp.float32
    ).astype(jnp.bfloat16)
    right_factor = jnp.einsum(
        "lesd,lkd->lesk", cotangents, project_out, preferred_element_type=jnp.float32
    )
    right_factor = jnp.where(live_mask[None, :, :, None], right_factor, 0.0).astype(jnp.bfloat16)
    partial_grad = jnp.einsum(
        "lesj,lesc->eljc", right_factor, left_factor, preferred_element_type=jnp.float32
    )
    partial_grad = partial_grad.reshape(partial_grad.shape[0], layer_count * block_size)
    grad_total = lax.psum(partial_grad, "mp")
    layer_place = mp_place // group_size
    grad_layer = lax.dynamic_slice_in_dim(
        grad_total, layer_place * block_size, block_size, 1
    ).astype(jnp.bfloat16)
    spread = lax.all_to_all(grad_layer, "dp", split_axis=1, concat_axis=0, tiled=True)
    partial_pre = lax.dot_general(
        spread, preconditioner, contract, preferred_element_type=jnp.float32
    )
    precond_grad = lax.psum(partial_pre, "dp")
    upper_grad, lower_grad = split_parts(precond_grad)
    scores = lax.psum_scatter(
        lax.dot_general(queries, upper_grad, contract, preferred_element_type=jnp.float32)
        + lax.dot_general(queries, lower_grad, contract, preferred_element_type=jnp.float32),
        "mp",
        scatter_dimension=0,
        tiled=True,
    )
    return scores.T


def body_direct(activations, cotangents, lengths, project_in, project_out, preconditioner, queries):
    layer_count = activations.shape[0]
    tokens_here = activations.shape[2]
    factor_size = project_in.shape[1]
    block_size = factor_size * factor_size
    width_dp = lax.axis_size("dp")
    mp_place = lax.axis_index("mp")
    partial_grad = layer_gradients(activations, cotangents, lengths, project_in, project_out)
    grad_mine = reduce_scatter_direct(partial_grad, "mp", 0)[0]
    grad_mine = grad_mine.astype(jnp.bfloat16).reshape(grad_mine.shape[0], block_size)
    grad_all = all_gather_a2a(grad_mine, "dp")
    grad_all = grad_all.reshape(-1, grad_all.shape[-1])
    copies = precondition(grad_all, preconditioner, width_dp)
    upper_grad, lower_grad = split_parts(lax.all_to_all(copies, "dp", 0, 0, tiled=True))
    both_all = jnp.concatenate([upper_grad, lower_grad], axis=1)
    blocks, block = both_all.shape[0], both_all.shape[2]
    query_blocks = queries.reshape(queries.shape[0], blocks, block)
    products = lax.dot_general(
        both_all, query_blocks, (((0, 2), (1, 2)), ((), ())), preferred_element_type=jnp.float32
    )
    examples = upper_grad.shape[1]
    partial_scores = products[:examples] + products[examples:]
    return reduce_scatter_direct(partial_scores, "mp", 1)


def body(*args):
    layer_count = args[0].shape[0]
    if lax.axis_size("mp") == layer_count:
        return body_direct(*args)
    return body_start(*args)


def solution(mesh):
    return jax.shard_map(
        body,
        mesh=mesh,
        in_specs=(
            P(None, "dp", "mp", None),
            P(None, "dp", "mp", None),
            P("dp"),
            P(),
            P(),
            P("mp", "dp"),
            P("dp", "mp"),
        ),
        out_specs=P(None, ("dp", "mp")),
        check_vma=False,
    )
```

```python
import jax
import jax.numpy as jnp
from jax import lax
from jax.experimental import pallas as pl
from jax.experimental.pallas import tpu as pltpu
from jax.sharding import PartitionSpec as P


def split_parts(dense):
    upper = dense.astype(jnp.bfloat16)
    kept = lax.optimization_barrier(upper)
    lower = (dense - kept.astype(jnp.float32)).astype(jnp.bfloat16)
    return (upper, lower)


def shifted(x, axis, shift):
    n = lax.axis_size(axis)
    return lax.ppermute(x, axis, [(i, (i + shift) % n) for i in range(n)])


def reduce_scatter_direct(x, axis, dim):
    n = lax.axis_size(axis)
    me = lax.axis_index(axis)
    width = x.shape[dim] // n
    total = lax.dynamic_slice_in_dim(x, me * width, width, dim)
    for shift in range(1, n):
        piece = lax.dynamic_slice_in_dim(x, ((me + shift) % n) * width, width, dim)
        total = total + shifted(piece, axis, shift)
    return total


def all_gather_direct(x, axis):
    n = lax.axis_size(axis)
    me = lax.axis_index(axis)
    got = [x] + [shifted(x, axis, shift) for shift in range(1, n)]
    order = jnp.stack([got[(-k) % n] for k in range(n)])
    doubled = jnp.concatenate([order, order], axis=0)
    return lax.dynamic_slice_in_dim(doubled, (n - me) % n, n, 0)


def all_gather_a2a(x, axis):
    n = lax.axis_size(axis)
    copies = jnp.broadcast_to(x[None], (n,) + x.shape)
    return lax.all_to_all(copies, axis, 0, 0, tiled=True)


def gradient_kernel(lengths_ref, act_ref, cot_ref, win_ref, wout_ref, *out_refs):
    step = pl.program_id(0)
    tokens = act_ref.shape[1]
    offset = lax.axis_index("mp") * tokens
    nt = (((1,), (1,)), ((), ()))
    grads = []
    for example in range(act_ref.shape[0]):
        left = lax.dot_general(
            act_ref[example], win_ref[...], nt, preferred_element_type=jnp.float32
        ).astype(jnp.bfloat16)
        right = lax.dot_general(
            cot_ref[example], wout_ref[...], nt, preferred_element_type=jnp.float32
        )
        rows = lax.broadcasted_iota(jnp.int32, right.shape, 0)
        right = jnp.where(rows < lengths_ref[example] - offset, right, 0.0).astype(jnp.bfloat16)
        grads.append(lax.dot_general(
            right, left, (((0,), (0,)), ((), ())), preferred_element_type=jnp.float32
        ))
    for index, out_ref in enumerate(out_refs):
        @pl.when(step == index)
        def _():
            for example, grad in enumerate(grads):
                out_ref[example] = grad


def layer_gradients(activations, cotangents, lengths, project_in, project_out):
    layers, examples, tokens, width = activations.shape
    factor = project_in.shape[1]

    def layer_of(t):
        return (lax.axis_index("mp") + 1 + t) % layers

    data = pl.BlockSpec((None, examples, tokens, width), lambda t, lens: (layer_of(t), 0, 0, 0))
    weights = pl.BlockSpec((None, factor, width), lambda t, lens: (layer_of(t), 0, 0))
    result = pl.BlockSpec((examples, factor, factor), lambda t, lens: (0, 0, 0))
    flops = 4 * layers * examples * tokens * width * factor
    moved = 2 * (activations.size + cotangents.size + project_in.size + project_out.size)
    return pl.pallas_call(
        gradient_kernel,
        out_shape=[jax.ShapeDtypeStruct((examples, factor, factor), jnp.float32)] * layers,
        grid_spec=pltpu.PrefetchScalarGridSpec(
            num_scalar_prefetch=1,
            grid=(layers,),
            in_specs=[data, data, weights, weights],
            out_specs=[result] * layers,
        ),
        cost_estimate=pl.CostEstimate(flops=flops, transcendentals=0, bytes_accessed=moved),
    )(lengths, activations, cotangents, project_in, project_out)


def body_start(activations, cotangents, lengths, project_in, project_out, preconditioner, queries):
    width_mp = lax.axis_size("mp")
    layer_count = activations.shape[0]
    tokens_here = activations.shape[2]
    factor_size = project_in.shape[1]
    block_size = factor_size * factor_size
    group_size = width_mp // layer_count
    mp_place = lax.axis_index("mp")
    contract = (((1,), (1,)), ((), ()))
    positions = mp_place * tokens_here + jnp.arange(tokens_here, dtype=jnp.int32)
    live_mask = positions[None, :] < lengths[:, None]
    left_factor = jnp.einsum(
        "lesd,lkd->lesk", activations, project_in, preferred_element_type=jnp.float32
    ).astype(jnp.bfloat16)
    right_factor = jnp.einsum(
        "lesd,lkd->lesk", cotangents, project_out, preferred_element_type=jnp.float32
    )
    right_factor = jnp.where(live_mask[None, :, :, None], right_factor, 0.0).astype(jnp.bfloat16)
    partial_grad = jnp.einsum(
        "lesj,lesc->eljc", right_factor, left_factor, preferred_element_type=jnp.float32
    )
    partial_grad = partial_grad.reshape(partial_grad.shape[0], layer_count * block_size)
    grad_total = lax.psum(partial_grad, "mp")
    layer_place = mp_place // group_size
    grad_layer = lax.dynamic_slice_in_dim(
        grad_total, layer_place * block_size, block_size, 1
    ).astype(jnp.bfloat16)
    spread = lax.all_to_all(grad_layer, "dp", split_axis=1, concat_axis=0, tiled=True)
    partial_pre = lax.dot_general(
        spread, preconditioner, contract, preferred_element_type=jnp.float32
    )
    precond_grad = lax.psum(partial_pre, "dp")
    upper_grad, lower_grad = split_parts(precond_grad)
    scores = lax.psum_scatter(
        lax.dot_general(queries, upper_grad, contract, preferred_element_type=jnp.float32)
        + lax.dot_general(queries, lower_grad, contract, preferred_element_type=jnp.float32),
        "mp",
        scatter_dimension=0,
        tiled=True,
    )
    return scores.T


def body_direct(activations, cotangents, lengths, project_in, project_out, preconditioner, queries):
    layer_count = activations.shape[0]
    tokens_here = activations.shape[2]
    factor_size = project_in.shape[1]
    block_size = factor_size * factor_size
    width_dp = lax.axis_size("dp")
    mp_place = lax.axis_index("mp")
    grads = layer_gradients(activations, cotangents, lengths, project_in, project_out)
    grad_mine = grads[-1]
    for shift in range(1, layer_count):
        grad_mine = grad_mine + shifted(grads[shift - 1], "mp", shift)
    grad_mine = grad_mine.astype(jnp.bfloat16).reshape(grad_mine.shape[0], block_size)
    grad_all = all_gather_a2a(grad_mine, "dp")
    grad_all = grad_all.reshape(-1, grad_all.shape[-1])
    pre_part = jnp.dot(grad_all, preconditioner, preferred_element_type=jnp.float32)
    upper_grad, lower_grad = split_parts(all_gather_a2a(pre_part, "dp"))
    both_all = jnp.concatenate([upper_grad, lower_grad], axis=1)
    blocks, block = both_all.shape[0], both_all.shape[2]
    query_blocks = queries.reshape(queries.shape[0], blocks, block)
    products = lax.dot_general(
        both_all, query_blocks, (((0, 2), (1, 2)), ((), ())), preferred_element_type=jnp.float32
    )
    examples = upper_grad.shape[1]
    partial_scores = products[:examples] + products[examples:]
    return reduce_scatter_direct(partial_scores, "mp", 1)


def body(*args):
    layer_count = args[0].shape[0]
    if lax.axis_size("mp") == layer_count:
        return body_direct(*args)
    return body_start(*args)


def solution(mesh):
    return jax.shard_map(
        body,
        mesh=mesh,
        in_specs=(
            P(None, "dp", "mp", None),
            P(None, "dp", "mp", None),
            P("dp"),
            P(),
            P(),
            P("mp", "dp"),
            P("dp", "mp"),
        ),
        out_specs=P(None, ("dp", "mp")),
        check_vma=False,
    )
```

```python
import jax
import jax.numpy as jnp
from jax import lax
from jax.experimental import pallas as pl
from jax.experimental.pallas import tpu as pltpu
from jax.sharding import PartitionSpec as P


def split_parts(dense):
    upper = dense.astype(jnp.bfloat16)
    kept = lax.optimization_barrier(upper)
    lower = (dense - kept.astype(jnp.float32)).astype(jnp.bfloat16)
    return (upper, lower)


def shifted(x, axis, shift):
    n = lax.axis_size(axis)
    return lax.ppermute(x, axis, [(i, (i + shift) % n) for i in range(n)])


def reduce_scatter_direct(x, axis, dim):
    n = lax.axis_size(axis)
    me = lax.axis_index(axis)
    width = x.shape[dim] // n
    total = lax.dynamic_slice_in_dim(x, me * width, width, dim)
    for shift in range(1, n):
        piece = lax.dynamic_slice_in_dim(x, ((me + shift) % n) * width, width, dim)
        total = total + shifted(piece, axis, shift)
    return total


def all_gather_direct(x, axis):
    n = lax.axis_size(axis)
    me = lax.axis_index(axis)
    got = [x] + [shifted(x, axis, shift) for shift in range(1, n)]
    order = jnp.stack([got[(-k) % n] for k in range(n)])
    doubled = jnp.concatenate([order, order], axis=0)
    return lax.dynamic_slice_in_dim(doubled, (n - me) % n, n, 0)


def all_gather_a2a(x, axis):
    n = lax.axis_size(axis)
    copies = jnp.broadcast_to(x[None], (n,) + x.shape)
    return lax.all_to_all(copies, axis, 0, 0, tiled=True)


def gradient_kernel(lengths_ref, act_ref, cot_ref, win_ref, wout_ref, out_ref):
    examples, tokens, width = act_ref.shape
    offset = lax.axis_index("mp") * tokens
    nt = (((1,), (1,)), ((), ()))
    left = lax.dot_general(
        act_ref[...].reshape(examples * tokens, width), win_ref[...], nt,
        preferred_element_type=jnp.float32,
    ).astype(jnp.bfloat16)
    right = lax.dot_general(
        cot_ref[...].reshape(examples * tokens, width), wout_ref[...], nt,
        preferred_element_type=jnp.float32,
    )
    rows = lax.broadcasted_iota(jnp.int32, (tokens, right.shape[1]), 0)
    for example in range(examples):
        rows_here = slice(example * tokens, (example + 1) * tokens)
        right_here = jnp.where(rows < lengths_ref[example] - offset, right[rows_here], 0.0)
        out_ref[example] = lax.dot_general(
            right_here.astype(jnp.bfloat16), left[rows_here], (((0,), (0,)), ((), ())),
            preferred_element_type=jnp.float32,
        )


def layer_gradients(activations, cotangents, lengths, project_in, project_out):
    layers, examples, tokens, width = activations.shape
    factor = project_in.shape[1]
    data = pl.BlockSpec((None, examples, tokens, width), lambda l, lens: (l, 0, 0, 0))
    weights = pl.BlockSpec((None, factor, width), lambda l, lens: (l, 0, 0))
    flops = 4 * layers * examples * tokens * width * factor
    moved = 2 * (activations.size + cotangents.size + project_in.size + project_out.size)
    return pl.pallas_call(
        gradient_kernel,
        out_shape=jax.ShapeDtypeStruct((layers, examples, factor, factor), jnp.float32),
        grid_spec=pltpu.PrefetchScalarGridSpec(
            num_scalar_prefetch=1,
            grid=(layers,),
            in_specs=[data, data, weights, weights],
            out_specs=pl.BlockSpec((None, examples, factor, factor), lambda l, lens: (l, 0, 0, 0)),
        ),
        cost_estimate=pl.CostEstimate(flops=flops, transcendentals=0, bytes_accessed=moved),
    )(lengths, activations, cotangents, project_in, project_out)


def body_start(activations, cotangents, lengths, project_in, project_out, preconditioner, queries):
    width_mp = lax.axis_size("mp")
    layer_count = activations.shape[0]
    tokens_here = activations.shape[2]
    factor_size = project_in.shape[1]
    block_size = factor_size * factor_size
    group_size = width_mp // layer_count
    mp_place = lax.axis_index("mp")
    contract = (((1,), (1,)), ((), ()))
    positions = mp_place * tokens_here + jnp.arange(tokens_here, dtype=jnp.int32)
    live_mask = positions[None, :] < lengths[:, None]
    left_factor = jnp.einsum(
        "lesd,lkd->lesk", activations, project_in, preferred_element_type=jnp.float32
    ).astype(jnp.bfloat16)
    right_factor = jnp.einsum(
        "lesd,lkd->lesk", cotangents, project_out, preferred_element_type=jnp.float32
    )
    right_factor = jnp.where(live_mask[None, :, :, None], right_factor, 0.0).astype(jnp.bfloat16)
    partial_grad = jnp.einsum(
        "lesj,lesc->eljc", right_factor, left_factor, preferred_element_type=jnp.float32
    )
    partial_grad = partial_grad.reshape(partial_grad.shape[0], layer_count * block_size)
    grad_total = lax.psum(partial_grad, "mp")
    layer_place = mp_place // group_size
    grad_layer = lax.dynamic_slice_in_dim(
        grad_total, layer_place * block_size, block_size, 1
    ).astype(jnp.bfloat16)
    spread = lax.all_to_all(grad_layer, "dp", split_axis=1, concat_axis=0, tiled=True)
    partial_pre = lax.dot_general(
        spread, preconditioner, contract, preferred_element_type=jnp.float32
    )
    precond_grad = lax.psum(partial_pre, "dp")
    upper_grad, lower_grad = split_parts(precond_grad)
    scores = lax.psum_scatter(
        lax.dot_general(queries, upper_grad, contract, preferred_element_type=jnp.float32)
        + lax.dot_general(queries, lower_grad, contract, preferred_element_type=jnp.float32),
        "mp",
        scatter_dimension=0,
        tiled=True,
    )
    return scores.T


def body_direct(activations, cotangents, lengths, project_in, project_out, preconditioner, queries):
    layer_count = activations.shape[0]
    tokens_here = activations.shape[2]
    factor_size = project_in.shape[1]
    block_size = factor_size * factor_size
    width_dp = lax.axis_size("dp")
    mp_place = lax.axis_index("mp")
    partial_grad = layer_gradients(activations, cotangents, lengths, project_in, project_out)
    grad_mine = reduce_scatter_direct(partial_grad, "mp", 0)[0]
    grad_mine = grad_mine.astype(jnp.bfloat16).reshape(grad_mine.shape[0], block_size)
    grad_all = all_gather_a2a(grad_mine, "dp")
    grad_all = grad_all.reshape(-1, grad_all.shape[-1])
    grad_copies = jnp.broadcast_to(grad_all[None], (width_dp,) + grad_all.shape)
    pre_copies = jnp.einsum(
        "nej,jc->nec", grad_copies, preconditioner, preferred_element_type=jnp.float32
    )
    upper_grad, lower_grad = split_parts(lax.all_to_all(pre_copies, "dp", 0, 0, tiled=True))
    both_all = jnp.concatenate([upper_grad, lower_grad], axis=1)
    blocks, block = both_all.shape[0], both_all.shape[2]
    query_blocks = queries.reshape(queries.shape[0], blocks, block)
    products = lax.dot_general(
        both_all, query_blocks, (((0, 2), (1, 2)), ((), ())), preferred_element_type=jnp.float32
    )
    examples = upper_grad.shape[1]
    partial_scores = products[:examples] + products[examples:]
    return reduce_scatter_direct(partial_scores, "mp", 1)


def body(*args):
    layer_count = args[0].shape[0]
    if lax.axis_size("mp") == layer_count:
        return body_direct(*args)
    return body_start(*args)


def solution(mesh):
    return jax.shard_map(
        body,
        mesh=mesh,
        in_specs=(
            P(None, "dp", "mp", None),
            P(None, "dp", "mp", None),
            P("dp"),
            P(),
            P(),
            P("mp", "dp"),
            P("dp", "mp"),
        ),
        out_specs=P(None, ("dp", "mp")),
        check_vma=False,
    )
```

```python
import jax
import jax.numpy as jnp
from jax import lax
from jax.experimental import pallas as pl
from jax.experimental.pallas import tpu as pltpu
from jax.sharding import PartitionSpec as P


def split_parts(dense):
    upper = dense.astype(jnp.bfloat16)
    kept = lax.optimization_barrier(upper)
    lower = (dense - kept.astype(jnp.float32)).astype(jnp.bfloat16)
    return (upper, lower)


def shifted(x, axis, shift):
    n = lax.axis_size(axis)
    return lax.ppermute(x, axis, [(i, (i + shift) % n) for i in range(n)])


def reduce_scatter_direct(x, axis, dim):
    n = lax.axis_size(axis)
    me = lax.axis_index(axis)
    width = x.shape[dim] // n
    total = lax.dynamic_slice_in_dim(x, me * width, width, dim)
    for shift in reversed(range(1, n)):
        piece = lax.dynamic_slice_in_dim(x, ((me + shift) % n) * width, width, dim)
        total = total + shifted(piece, axis, shift)
    return total


def all_gather_direct(x, axis):
    n = lax.axis_size(axis)
    me = lax.axis_index(axis)
    got = [x] + [shifted(x, axis, shift) for shift in range(1, n)]
    order = jnp.stack([got[(-k) % n] for k in range(n)])
    doubled = jnp.concatenate([order, order], axis=0)
    return lax.dynamic_slice_in_dim(doubled, (n - me) % n, n, 0)


def all_gather_a2a(x, axis):
    n = lax.axis_size(axis)
    copies = jnp.broadcast_to(x[None], (n,) + x.shape)
    return lax.all_to_all(copies, axis, 0, 0, tiled=True)


def gradient_kernel(lengths_ref, act_ref, cot_ref, win_ref, wout_ref, out_ref):
    examples, tokens, width = act_ref.shape
    offset = lax.axis_index("mp") * tokens
    nt = (((1,), (1,)), ((), ()))
    left = lax.dot_general(
        act_ref[...].reshape(examples * tokens, width), win_ref[...], nt,
        preferred_element_type=jnp.float32,
    ).astype(jnp.bfloat16)
    right = lax.dot_general(
        cot_ref[...].reshape(examples * tokens, width), wout_ref[...], nt,
        preferred_element_type=jnp.float32,
    )
    rows = lax.broadcasted_iota(jnp.int32, (tokens, right.shape[1]), 0)
    for example in range(examples):
        rows_here = slice(example * tokens, (example + 1) * tokens)
        right_here = jnp.where(rows < lengths_ref[example] - offset, right[rows_here], 0.0)
        out_ref[example] = lax.dot_general(
            right_here.astype(jnp.bfloat16), left[rows_here], (((0,), (0,)), ((), ())),
            preferred_element_type=jnp.float32,
        )


def layer_gradients(activations, cotangents, lengths, project_in, project_out):
    layers, examples, tokens, width = activations.shape
    factor = project_in.shape[1]
    data = pl.BlockSpec((None, examples, tokens, width), lambda l, lens: (l, 0, 0, 0))
    weights = pl.BlockSpec((None, factor, width), lambda l, lens: (l, 0, 0))
    flops = 4 * layers * examples * tokens * width * factor
    moved = 2 * (activations.size + cotangents.size + project_in.size + project_out.size)
    return pl.pallas_call(
        gradient_kernel,
        out_shape=jax.ShapeDtypeStruct((layers, examples, factor, factor), jnp.float32),
        grid_spec=pltpu.PrefetchScalarGridSpec(
            num_scalar_prefetch=1,
            grid=(layers,),
            in_specs=[data, data, weights, weights],
            out_specs=pl.BlockSpec((None, examples, factor, factor), lambda l, lens: (l, 0, 0, 0)),
        ),
        cost_estimate=pl.CostEstimate(flops=flops, transcendentals=0, bytes_accessed=moved),
    )(lengths, activations, cotangents, project_in, project_out)


def body_start(activations, cotangents, lengths, project_in, project_out, preconditioner, queries):
    width_mp = lax.axis_size("mp")
    layer_count = activations.shape[0]
    tokens_here = activations.shape[2]
    factor_size = project_in.shape[1]
    block_size = factor_size * factor_size
    group_size = width_mp // layer_count
    mp_place = lax.axis_index("mp")
    contract = (((1,), (1,)), ((), ()))
    positions = mp_place * tokens_here + jnp.arange(tokens_here, dtype=jnp.int32)
    live_mask = positions[None, :] < lengths[:, None]
    left_factor = jnp.einsum(
        "lesd,lkd->lesk", activations, project_in, preferred_element_type=jnp.float32
    ).astype(jnp.bfloat16)
    right_factor = jnp.einsum(
        "lesd,lkd->lesk", cotangents, project_out, preferred_element_type=jnp.float32
    )
    right_factor = jnp.where(live_mask[None, :, :, None], right_factor, 0.0).astype(jnp.bfloat16)
    partial_grad = jnp.einsum(
        "lesj,lesc->eljc", right_factor, left_factor, preferred_element_type=jnp.float32
    )
    partial_grad = partial_grad.reshape(partial_grad.shape[0], layer_count * block_size)
    grad_total = lax.psum(partial_grad, "mp")
    layer_place = mp_place // group_size
    grad_layer = lax.dynamic_slice_in_dim(
        grad_total, layer_place * block_size, block_size, 1
    ).astype(jnp.bfloat16)
    spread = lax.all_to_all(grad_layer, "dp", split_axis=1, concat_axis=0, tiled=True)
    partial_pre = lax.dot_general(
        spread, preconditioner, contract, preferred_element_type=jnp.float32
    )
    precond_grad = lax.psum(partial_pre, "dp")
    upper_grad, lower_grad = split_parts(precond_grad)
    scores = lax.psum_scatter(
        lax.dot_general(queries, upper_grad, contract, preferred_element_type=jnp.float32)
        + lax.dot_general(queries, lower_grad, contract, preferred_element_type=jnp.float32),
        "mp",
        scatter_dimension=0,
        tiled=True,
    )
    return scores.T


def body_direct(activations, cotangents, lengths, project_in, project_out, preconditioner, queries):
    layer_count = activations.shape[0]
    tokens_here = activations.shape[2]
    factor_size = project_in.shape[1]
    block_size = factor_size * factor_size
    width_dp = lax.axis_size("dp")
    mp_place = lax.axis_index("mp")
    partial_grad = layer_gradients(activations, cotangents, lengths, project_in, project_out)
    grad_mine = reduce_scatter_direct(partial_grad, "mp", 0)[0]
    grad_mine = grad_mine.astype(jnp.bfloat16).reshape(grad_mine.shape[0], block_size)
    grad_all = all_gather_a2a(grad_mine, "dp")
    grad_all = grad_all.reshape(-1, grad_all.shape[-1])
    grad_copies = jnp.broadcast_to(grad_all[None], (width_dp,) + grad_all.shape)
    pre_copies = jnp.einsum(
        "nej,jc->nec", grad_copies, preconditioner, preferred_element_type=jnp.float32
    )
    upper_grad, lower_grad = split_parts(lax.all_to_all(pre_copies, "dp", 0, 0, tiled=True))
    both_all = jnp.concatenate([upper_grad, lower_grad], axis=1)
    blocks, block = both_all.shape[0], both_all.shape[2]
    query_blocks = queries.reshape(queries.shape[0], blocks, block)
    products = lax.dot_general(
        both_all, query_blocks, (((0, 2), (1, 2)), ((), ())), preferred_element_type=jnp.float32
    )
    examples = upper_grad.shape[1]
    partial_scores = products[:examples] + products[examples:]
    return reduce_scatter_direct(partial_scores, "mp", 1)


def body(*args):
    layer_count = args[0].shape[0]
    if lax.axis_size("mp") == layer_count:
        return body_direct(*args)
    return body_start(*args)


def solution(mesh):
    return jax.shard_map(
        body,
        mesh=mesh,
        in_specs=(
            P(None, "dp", "mp", None),
            P(None, "dp", "mp", None),
            P("dp"),
            P(),
            P(),
            P("mp", "dp"),
            P("dp", "mp"),
        ),
        out_specs=P(None, ("dp", "mp")),
        check_vma=False,
    )
```
